128 devices in a mesh: seq: 4 (over x), exp: 32 (over y, z, core).
Axes of the slice: x: 4, y: 4, z: 4, core: 2. Of those that a mesh axis runs over, the one named last changes fastest.
Arguments:
- resid: bfloat16 [32, 384, 2048], P('exp', 'seq'), may hold values from -6 to 6
- qkv: bfloat16 [32, 384, 6144], P('exp', 'seq'), may hold values from -8 to 8
- w_out: bfloat16 [2048, 2048], P('seq'), may hold values from -0.125 to 0.125
- norm_gain: float32 [2048], replicated, may hold values from 0.1 to 1.9
- router_w: bfloat16 [2048, 64], replicated, may hold values from -0.125 to 0.125
- expert_ids: int32 [32, 384, 6], P('exp'), may hold values from 0 to 63, all different within a row; in each aligned block of 96 rows (0 to 95, 96 to 191, ..., all dimensions but the last counted through in order) at most 12 rows name the same one
- w_gate_up: bfloat16 [64, 2048, 2, 1408], P('exp', None, None, 'seq'), may hold values from -0.125 to 0.125
- w_down: bfloat16 [64, 1408, 2048], P('exp', 'seq'), may hold values from -0.15625 to 0.15625
Outputs:
- layer_out: bfloat16 [32, 384, 2048], P('exp', 'seq')
The draws below stay inside these ranges and needn't reach their ends.
Inputs may be any that keep to these rules, and one draw needn't show every extreme that they name: `expert_ids`: each point names 6 different experts. In each aligned block of 96 points (the points of one device, in the order of sets and then points), no expert is named by more than 12 points, and in every draw some expert is named by exactly 12 points of some block.
All inputs are finite; a program needn't handle non-finite values.
Results may differ from the reference program's by a relative error of at most 0.0065.
Values may be sent and summed in bfloat16 or wider, within the bound.
No kernel may reach another device: no remote copies, remote signals or barrier semaphores. Data moves between devices by JAX's collectives and lax.ppermute only.
A program may use at most 128 MiB of HBM per device.

```python
import math
import jax
import jax.numpy as jnp
import numpy as np
from jax import lax

D = 2048
H = 16
HD = 128
FF = 1408
EXPERTS = 64
TOPK = 6
TOK_DEV = 96
SET_LEN = 384
SETS = 32
SLOTS = 12
N_SEQ = 4


def draw_qkv(key, part):
    base = jnp.clip(jax.random.normal(key, (SETS, SET_LEN, 3, D), jnp.float32), -8.0, 8.0)
    return base.reshape(SETS, SET_LEN, 3 * D).astype(jnp.bfloat16)


def level_of(stream_key, dims, shards, low, top_value):
    factor_of = 1.0
    for axis_at, blocks in shards:
        draws = jax.random.uniform(jax.random.fold_in(jax.random.fold_in(stream_key, 6), axis_at), (blocks,), jnp.float32, low / len(shards), top_value / len(shards))
        factor_of = factor_of * jnp.repeat(jnp.exp(draws), dims[axis_at] // blocks).reshape((-1,) + (1,) * (len(dims) - 1 - axis_at))
    return factor_of


def routed_block(stream_key, own, number, rows, number_of, top, limit, slope):
    ranking = jax.random.permutation(stream_key, number_of)
    crowded, common = load_shares(number_of, rows * top, limit, slope, True), load_shares(number_of, rows * top, limit, slope, False)
    places = jnp.arange(number_of)

    def named(sizes, offset_by):
        used = int((sizes > 0).sum())
        fixed = max(1, used // 4)
        moved = fixed + (places - fixed + offset_by * (used - fixed)) % max(1, number_of - fixed)
        return jnp.zeros((number_of,), jnp.int32).at[ranking[jnp.where(places < fixed, places, moved)]].set(jnp.asarray(sizes, jnp.int32))

    sizes = jnp.where(number % 4 == 0, named(crowded, number // 4), named(common, number - number // 4 - 1))
    mixed = jax.random.permutation(jax.random.fold_in(own, 3), number_of)
    giver, receiver = mixed[0:number_of // 2 * 2:2], mixed[1:number_of // 2 * 2:2]
    slack = jnp.minimum(sizes[giver] - 1, limit - sizes[receiver]) // 2
    slack = jnp.where((giver == ranking[0]) | (receiver == ranking[0]) | (sizes[receiver] == 0), 0, jnp.maximum(slack, 0))
    moved = jax.random.randint(jax.random.fold_in(own, 4), (number_of // 2,), 0, 1 << 20) % (slack + 1)
    sizes = sizes.at[giver].add(-moved).at[receiver].add(moved)
    labels = jnp.searchsorted(jnp.cumsum(sizes), jnp.arange(rows * top), side="right").astype(jnp.int32)
    grid = labels.reshape(top, rows).T
    grid = grid[jax.random.permutation(jax.random.fold_in(own, 1), rows)]
    offset_by = jax.random.randint(jax.random.fold_in(own, 2), (rows, 1), 0, top)
    return jnp.take_along_axis(grid, (jnp.arange(top)[None, :] + offset_by) % top, axis=1)


def load_shares(count, total, most, slope, full):
    loads = [(1 << 20) // math.isqrt(standing ** slope) + 1 for standing in range(1, count + 1)]
    largest = most if full else min(most, max(-(-total // count), total * loads[0] // sum(loads)))
    least = 1 if total - largest >= count - 1 else 0
    counts, surplus = [largest] + [least] * (count - 1), total - largest - least * (count - 1)
    while surplus > 0:
        free = [i for i in range(1, count) if counts[i] < largest] or [i for i in range(1, count) if counts[i] < most]
        whole, remaining = sum([loads[i] for i in free]), surplus
        for i in free:
            more = min(most - counts[i], max(1, remaining * loads[i] // whole), surplus)
            counts[i] = counts[i] + more
            surplus = surplus - more
    return np.array(counts)


def normal_values(key, dims, scale, limit, split=(), kind=jnp.bfloat16):
    factor_of = level_of(key, dims, split, -0.22, 0.18) if split else 1.0
    result = jax.random.normal(key, dims, jnp.float32) * scale * factor_of
    return jnp.minimum(jnp.maximum(result, -limit), limit).astype(kind)


def setup_inputs(seed: int = 0) -> dict:
    key_of = jax.random.split(jax.random.key(seed), 9)
    resid = normal_values(key_of[0], (SETS, SET_LEN, D), 1.0, 6.0, ((0, 32), (1, 4)))
    qkv = draw_qkv(jax.random.fold_in(key_of[8], 71), 0)
    w_out = normal_values(key_of[2], (D, D), D ** -0.5, 0.125, ((0, 4),))
    norm_gain = jnp.clip(1.0 + 0.18 * jax.random.normal(key_of[3], (D,), jnp.float32), 0.1, 1.9)
    router_w = normal_values(key_of[4], (D, EXPERTS), D ** -0.5, 0.125)
    expert_ids_keys = jax.random.split(jax.random.fold_in(key_of[5], 1), SETS * SET_LEN // TOK_DEV)
    expert_ids_turns = jax.random.permutation(jax.random.fold_in(key_of[5], 3), SETS * SET_LEN // TOK_DEV)
    expert_ids = jax.vmap(lambda own, number: routed_block(jax.random.fold_in(key_of[5], 2), own, number, TOK_DEV, EXPERTS, TOPK, SLOTS, 2))(expert_ids_keys, expert_ids_turns).reshape((SETS, SET_LEN, TOPK))
    w_gate_up = normal_values(key_of[6], (EXPERTS, D, 2, FF), D ** -0.5, 0.125, ((0, 32), (3, 4)))
    w_down = normal_values(key_of[7], (EXPERTS, FF, D), FF ** -0.5, 0.15625, ((0, 32), (1, 4)))
    return {"resid": resid, "qkv": qkv, "w_out": w_out, "norm_gain": norm_gain, "router_w": router_w, "expert_ids": expert_ids, "w_gate_up": w_gate_up, "w_down": w_down}


epsilon = 1e-05

def gate_weights(normed_rows, router_w, chosen):
    logits = jnp.dot(normed_rows, router_w, preferred_element_type=jnp.float32)
    match = chosen[:, :, None] == jnp.arange(logits.shape[1], dtype=jnp.int32)[None, None, :]
    picked = lax.optimization_barrier(jnp.sum(jnp.where(match, logits[:, None, :], jnp.zeros((), logits.dtype)), axis=-1))
    squashed = jax.nn.sigmoid(picked)
    return squashed / lax.optimization_barrier(jnp.sum(squashed, axis=-1, keepdims=True))

def slot_ranks(chosen, block_rows, experts):
    blocks = chosen.shape[0] // block_rows
    grouped = chosen.reshape(blocks, block_rows * chosen.shape[1])
    hits = (grouped[:, :, None] == jnp.arange(experts, dtype=jnp.int32)[None, None, :]).astype(jnp.int32)
    ranks = lax.optimization_barrier(jnp.sum(jnp.cumsum(hits, axis=1) * hits, axis=-1)) - 1
    return ranks.reshape(chosen.shape).astype(jnp.int32)

def attend(set_block):
    parts = set_block.reshape(SET_LEN, 3, H, HD).astype(jnp.float32)
    scores = jnp.einsum('qhd,khd->hqk', parts[:, 0], parts[:, 1]) / math.sqrt(HD)
    rounded = jax.nn.softmax(scores, axis=-1).astype(jnp.bfloat16)
    weights = lax.optimization_barrier(rounded).astype(jnp.float32)
    mixed = jnp.einsum('hqk,khd->qhd', weights, parts[:, 2])
    return mixed.reshape(SET_LEN, D).astype(jnp.bfloat16)

def expert_out(packed):
    inputs, gate_up, down = packed
    count_rows = inputs.shape[0]
    both = jnp.dot(inputs, gate_up.reshape(D, 2 * FF), preferred_element_type=jnp.float32).reshape(count_rows, 2, FF)
    hidden = (jax.nn.silu(both[:, 0]) * both[:, 1]).astype(jnp.bfloat16)
    block_units = FF // N_SEQ
    running = jnp.zeros((count_rows, D), jnp.float32)
    for quarter in range(N_SEQ):
        lower = quarter * block_units
        part_out = jnp.dot(hidden[:, lower:lower + block_units], down[lower:lower + block_units], preferred_element_type=jnp.float32).astype(jnp.bfloat16)
        running = running + lax.optimization_barrier(part_out).astype(jnp.float32)
    return running

def reference(resid, qkv, w_out, norm_gain, router_w, expert_ids, w_gate_up, w_down):
    attended = lax.map(attend, qkv).reshape(-1, D)
    mixed = resid.reshape(-1, D).astype(jnp.float32) + jnp.dot(attended, w_out, preferred_element_type=jnp.float32)
    meansq = lax.optimization_barrier(jnp.mean(mixed * mixed, axis=-1, keepdims=True))
    normed = (mixed * lax.rsqrt(meansq + epsilon) * norm_gain).astype(jnp.bfloat16)
    chosen = expert_ids.reshape(-1, TOPK)
    gate_vals = gate_weights(normed, router_w, chosen)
    point_count = chosen.shape[0]
    blocks = point_count // TOK_DEV
    ranks = slot_ranks(chosen, TOK_DEV, EXPERTS)
    source_block = (jnp.arange(point_count, dtype=jnp.int32) // TOK_DEV)[:, None]
    slot_index = chosen * (blocks * SLOTS) + source_block * SLOTS + ranks
    spread = jnp.broadcast_to(normed[:, None, :], (point_count, TOPK, D)).reshape(-1, D)
    buffers = jnp.zeros((EXPERTS * blocks * SLOTS, D), jnp.bfloat16).at[slot_index.reshape(-1)].set(spread)
    outputs = lax.map(expert_out, (buffers.reshape(EXPERTS, blocks * SLOTS, D), w_gate_up, w_down))
    out_table = outputs.reshape(-1, D)
    expert_sum = lax.optimization_barrier(jnp.sum(gate_vals[:, :, None] * out_table[slot_index], axis=1))
    return (mixed + expert_sum).astype(jnp.bfloat16).reshape(SETS, SET_LEN, D)
```

```python
import math

import jax
import jax.numpy as jnp
from jax import lax
from jax.sharding import PartitionSpec as P

H = 16
HD = 128
EXPERTS = 64


epsilon = 1e-05


def gate_weights(normed_rows, router_w, chosen):
    logits = jnp.dot(normed_rows, router_w, preferred_element_type=jnp.float32)
    match = chosen[:, :, None] == jnp.arange(logits.shape[1], dtype=jnp.int32)[None, None, :]
    picked = jnp.sum(jnp.where(match, logits[:, None, :], jnp.zeros((), logits.dtype)), axis=-1)
    squashed = jax.nn.sigmoid(picked)
    return squashed / jnp.sum(squashed, axis=-1, keepdims=True)


def slot_ranks(chosen, block_rows, experts):
    blocks = chosen.shape[0] // block_rows
    width = block_rows * chosen.shape[1]
    grouped = chosen.reshape(blocks, width)
    hits = (grouped[:, :, None] == jnp.arange(experts, dtype=jnp.int32)[None, None, :]).astype(
        jnp.bfloat16
    )
    lower = jnp.arange(width)[:, None] >= jnp.arange(width)[None, :]
    counts = jnp.einsum(
        "ij,bje->bie", lower.astype(jnp.bfloat16), hits, preferred_element_type=jnp.float32
    )
    ranks = jnp.sum(counts * hits.astype(jnp.float32), axis=-1) - 1
    return ranks.astype(jnp.int32).reshape(chosen.shape)


def expert_part(received, w_gate_up, w_down):
    both = jnp.einsum("aend,edgf->aengf", received, w_gate_up, preferred_element_type=jnp.float32)
    hidden = (jax.nn.silu(both[:, :, :, 0]) * both[:, :, :, 1]).astype(jnp.bfloat16)
    return jnp.einsum("aenf,efd->aend", hidden, w_down, preferred_element_type=jnp.float32)


def scatter_rows(normed_rows, slot_index, buffer_rows):
    slots = jnp.arange(buffer_rows, dtype=jnp.int32)
    select = jnp.sum(
        (slot_index[None, :, :] == slots[:, None, None]).astype(jnp.bfloat16), axis=-1
    )
    return jnp.dot(select, normed_rows, preferred_element_type=jnp.float32).astype(jnp.bfloat16)


def combine_rows(out_table, slot_index, gate_vals):
    slots = jnp.arange(out_table.shape[0], dtype=jnp.int32)
    weights = jnp.sum(
        jnp.where(slot_index[:, :, None] == slots[None, None, :], gate_vals[:, :, None], 0.0),
        axis=1,
    )
    high = weights.astype(jnp.bfloat16)
    low = (weights - high.astype(jnp.float32)).astype(jnp.bfloat16)
    return jnp.dot(high, out_table, preferred_element_type=jnp.float32) + jnp.dot(
        low, out_table, preferred_element_type=jnp.float32
    )


def on_device(resid, qkv, w_out, norm_gain, router_w, expert_ids, w_gate_up, w_down):
    row_count = resid.shape[1]
    model_width = resid.shape[2]
    seq_size = lax.axis_size("seq")
    exp_size = lax.axis_size("exp")
    seq_length = row_count * seq_size
    head_local = H // seq_size
    local_width = head_local * HD
    packed = qkv.reshape(row_count, 3, seq_size, local_width)
    regrouped = lax.all_to_all(packed, "seq", split_axis=2, concat_axis=0, tiled=True)
    queries = regrouped[:, 0, 0].reshape(seq_length, head_local, HD)
    keys_all = regrouped[:, 1, 0].reshape(seq_length, head_local, HD)
    values_all = regrouped[:, 2, 0].reshape(seq_length, head_local, HD)
    query_block = min(seq_length, 512)

    def attend_block(query_rows):
        scores = jnp.einsum(
            "qhd,khd->hqk", query_rows, keys_all, preferred_element_type=jnp.float32
        ) / math.sqrt(HD)
        weights = jax.nn.softmax(scores, axis=-1).astype(jnp.bfloat16)
        mixed_heads = jnp.einsum(
            "hqk,khd->qhd", weights, values_all, preferred_element_type=jnp.float32
        )
        return mixed_heads.reshape(query_rows.shape[0], local_width).astype(jnp.bfloat16)

    attended = lax.map(
        attend_block, queries.reshape(seq_length // query_block, query_block, head_local, HD)
    )
    attended = attended.reshape(seq_length, local_width)
    back = lax.all_to_all(
        attended.reshape(seq_length, 1, local_width), "seq", split_axis=0, concat_axis=1, tiled=True
    )
    point_rows = back.reshape(row_count, model_width)
    projected = jnp.dot(
        point_rows,
        lax.all_gather(w_out, "seq", axis=0, tiled=True),
        preferred_element_type=jnp.float32,
    )
    mixed = resid[0].astype(jnp.float32) + projected
    meansq = jnp.mean(mixed * mixed, axis=-1, keepdims=True)
    normed = (mixed * lax.rsqrt(meansq + epsilon) * norm_gain).astype(jnp.bfloat16)
    exp_local = w_gate_up.shape[0]
    slot_cap = row_count // 8
    gathered = lax.all_gather(normed, "seq", axis=0, tiled=True)
    chosen = expert_ids[0]
    gate_vals = gate_weights(gathered, router_w, chosen)
    ranks = slot_ranks(chosen, row_count, EXPERTS)
    owner_rows = seq_size * slot_cap
    source_block = (jnp.arange(seq_length, dtype=jnp.int32) // row_count)[:, None]
    slot_index = chosen * owner_rows + source_block * slot_cap + ranks
    outgoing = scatter_rows(gathered, slot_index, EXPERTS * owner_rows)
    outgoing = outgoing.reshape(exp_size, exp_local, owner_rows, model_width)
    partial_out = expert_part(
        lax.all_to_all(outgoing, "exp", split_axis=0, concat_axis=0, tiled=True), w_gate_up, w_down
    ).astype(jnp.bfloat16)
    returned = lax.all_to_all(partial_out, "exp", split_axis=0, concat_axis=0, tiled=True)
    out_table = returned.reshape(-1, model_width)
    expert_sum = lax.psum_scatter(
        combine_rows(out_table, slot_index, gate_vals).astype(jnp.bfloat16),
        "seq",
        scatter_dimension=0,
        tiled=True,
    ).astype(jnp.float32)
    return (mixed + expert_sum).astype(jnp.bfloat16).reshape(1, row_count, model_width)


def solution(mesh):
    in_specs = (
        P("exp", "seq", None),
        P("exp", "seq", None),
        P("seq", None),
        P(),
        P(),
        P("exp", None, None),
        P("exp", None, None, "seq"),
        P("exp", "seq", None),
    )
    out_specs = P("exp", "seq", None)
    return jax.shard_map(
        on_device, mesh=mesh, in_specs=in_specs, out_specs=out_specs, check_vma=False
    )
```

```python
import math

import jax
import jax.numpy as jnp
from jax import lax
from jax.sharding import PartitionSpec as P

H = 16
HD = 128
EXPERTS = 64


epsilon = 1e-05


def gate_weights(normed_rows, router_w, chosen):
    logits = jnp.dot(normed_rows, router_w, preferred_element_type=jnp.float32)
    match = chosen[:, :, None] == jnp.arange(logits.shape[1], dtype=jnp.int32)[None, None, :]
    picked = jnp.sum(jnp.where(match, logits[:, None, :], jnp.zeros((), logits.dtype)), axis=-1)
    squashed = jax.nn.sigmoid(picked)
    return squashed / jnp.sum(squashed, axis=-1, keepdims=True)


def slot_ranks(chosen, block_rows, experts):
    blocks = chosen.shape[0] // block_rows
    width = block_rows * chosen.shape[1]
    grouped = chosen.reshape(blocks, width)
    hits = (grouped[:, :, None] == jnp.arange(experts, dtype=jnp.int32)[None, None, :]).astype(
        jnp.bfloat16
    )
    lower = jnp.arange(width)[:, None] >= jnp.arange(width)[None, :]
    counts = jnp.einsum(
        "ij,bje->bie", lower.astype(jnp.bfloat16), hits, preferred_element_type=jnp.float32
    )
    ranks = jnp.sum(counts * hits.astype(jnp.float32), axis=-1) - 1
    return ranks.astype(jnp.int32).reshape(chosen.shape)


def expert_part(received, w_gate_up, w_down):
    both = jnp.einsum("aend,edgf->aengf", received, w_gate_up, preferred_element_type=jnp.float32)
    hidden = (jax.nn.silu(both[:, :, :, 0]) * both[:, :, :, 1]).astype(jnp.bfloat16)
    return jnp.einsum("aenf,efd->aend", hidden, w_down, preferred_element_type=jnp.float32)


def scatter_rows(normed_rows, slot_index, buffer_rows):
    slots = jnp.arange(buffer_rows, dtype=jnp.int32)
    select = jnp.sum(
        (slot_index[None, :, :] == slots[:, None, None]).astype(jnp.bfloat16), axis=-1
    )
    return jnp.dot(select, normed_rows, preferred_element_type=jnp.float32).astype(jnp.bfloat16)


def combine_rows(out_table, slot_index, gate_vals):
    slots = jnp.arange(out_table.shape[0], dtype=jnp.int32)
    weights = jnp.sum(
        jnp.where(slot_index[:, :, None] == slots[None, None, :], gate_vals[:, :, None], 0.0),
        axis=1,
    )
    high = weights.astype(jnp.bfloat16)
    low = (weights - high.astype(jnp.float32)).astype(jnp.bfloat16)
    return jnp.dot(high, out_table, preferred_element_type=jnp.float32) + jnp.dot(
        low, out_table, preferred_element_type=jnp.float32
    )


def seq_shift(x, shift, size):
    return lax.ppermute(x, "seq", [(i, (i + shift) % size) for i in range(size)])


def on_device(resid, qkv, w_out, norm_gain, router_w, expert_ids, w_gate_up, w_down):
    row_count = resid.shape[1]
    model_width = resid.shape[2]
    seq_size = lax.axis_size("seq")
    exp_size = lax.axis_size("exp")
    me = lax.axis_index("seq")
    seq_length = row_count * seq_size
    head_local = H // seq_size
    local_width = head_local * HD
    packed = qkv[0].reshape(row_count, 3, seq_size, local_width)
    pieces = []
    for shift in range(seq_size):
        target = (me + shift) % seq_size
        piece = lax.dynamic_index_in_dim(packed, target, axis=2, keepdims=False)
        pieces.append(piece if shift == 0 else seq_shift(piece, shift, seq_size))
    regrouped = jnp.stack(pieces, axis=0).reshape(seq_length, 3, local_width)
    queries = regrouped[:, 0].reshape(seq_length, head_local, HD)
    keys_all = regrouped[:, 1].reshape(seq_length, head_local, HD)
    values_all = regrouped[:, 2].reshape(seq_length, head_local, HD)
    scores = jnp.einsum(
        "qhd,khd->hqk", queries, keys_all, preferred_element_type=jnp.float32
    ) / math.sqrt(HD)
    weights = jax.nn.softmax(scores, axis=-1).astype(jnp.bfloat16)
    attended = jnp.einsum(
        "hqk,khd->qhd", weights, values_all, preferred_element_type=jnp.float32
    ).reshape(seq_length, local_width).astype(jnp.bfloat16)
    partial = jnp.dot(attended, w_out, preferred_element_type=jnp.float32).reshape(
        seq_size, row_count, model_width
    )
    projected = partial[0]
    for shift in range(1, seq_size):
        projected = projected + seq_shift(partial[shift], -shift, seq_size)
    mixed = resid[0].astype(jnp.float32) + projected
    meansq = jnp.mean(mixed * mixed, axis=-1, keepdims=True)
    normed = (mixed * lax.rsqrt(meansq + epsilon) * norm_gain).astype(jnp.bfloat16)
    exp_local = w_gate_up.shape[0]
    slot_cap = row_count // 8
    gathered = jnp.concatenate(
        [normed] + [seq_shift(normed, shift, seq_size) for shift in range(1, seq_size)], axis=0
    )
    blocks_abs = (me - jnp.arange(seq_size, dtype=jnp.int32)) % seq_size
    chosen = jnp.take(expert_ids[0].reshape(seq_size, row_count, -1), blocks_abs, axis=0).reshape(
        seq_length, -1
    )
    gate_vals = gate_weights(gathered, router_w, chosen)
    ranks = slot_ranks(chosen, row_count, EXPERTS)
    owner_rows = seq_size * slot_cap
    source_block = jnp.repeat(blocks_abs, row_count)[:, None]
    slot_index = chosen * owner_rows + source_block * slot_cap + ranks
    outgoing = scatter_rows(gathered, slot_index, EXPERTS * owner_rows)
    outgoing = outgoing.reshape(exp_size, exp_local, owner_rows, model_width)
    partial_out = expert_part(
        lax.all_to_all(outgoing, "exp", split_axis=0, concat_axis=0, tiled=True), w_gate_up, w_down
    ).astype(jnp.bfloat16)
    returned = lax.all_to_all(partial_out, "exp", split_axis=0, concat_axis=0, tiled=True)
    out_table = returned.reshape(-1, model_width)
    combined = combine_rows(out_table, slot_index, gate_vals).reshape(
        seq_size, row_count, model_width
    )
    expert_sum = combined[0]
    for shift in range(1, seq_size):
        expert_sum = expert_sum + seq_shift(
            combined[shift].astype(jnp.bfloat16), -shift, seq_size
        ).astype(jnp.float32)
    return (mixed + expert_sum).astype(jnp.bfloat16).reshape(1, row_count, model_width)


def solution(mesh):
    in_specs = (
        P("exp", "seq", None),
        P("exp", "seq", None),
        P("seq", None),
        P(),
        P(),
        P("exp", None, None),
        P("exp", None, None, "seq"),
        P("exp", "seq", None),
    )
    out_specs = P("exp", "seq", None)
    return jax.shard_map(
        on_device, mesh=mesh, in_specs=in_specs, out_specs=out_specs, check_vma=False
    )
```

```python
import math

import jax
import jax.numpy as jnp
from jax import lax
from jax.sharding import PartitionSpec as P

H = 16
HD = 128
EXPERTS = 64


epsilon = 1e-05


def gate_weights(normed_rows, router_w, chosen):
    logits = jnp.dot(normed_rows, router_w, preferred_element_type=jnp.float32)
    match = chosen[:, :, None] == jnp.arange(logits.shape[1], dtype=jnp.int32)[None, None, :]
    picked = jnp.sum(jnp.where(match, logits[:, None, :], jnp.zeros((), logits.dtype)), axis=-1)
    squashed = jax.nn.sigmoid(picked)
    return squashed / jnp.sum(squashed, axis=-1, keepdims=True)


def slot_ranks(chosen, block_rows, experts):
    blocks = chosen.shape[0] // block_rows
    width = block_rows * chosen.shape[1]
    grouped = chosen.reshape(blocks, width)
    hits = (grouped[:, :, None] == jnp.arange(experts, dtype=jnp.int32)[None, None, :]).astype(
        jnp.bfloat16
    )
    lower = jnp.arange(width)[:, None] >= jnp.arange(width)[None, :]
    counts = jnp.einsum(
        "ij,bje->bie", lower.astype(jnp.bfloat16), hits, preferred_element_type=jnp.float32
    )
    ranks = jnp.sum(counts * hits.astype(jnp.float32), axis=-1) - 1
    return ranks.astype(jnp.int32).reshape(chosen.shape)


def expert_one(rows, gate_up, down):
    both = jnp.einsum("nd,dgf->ngf", rows, gate_up, preferred_element_type=jnp.float32)
    hidden = (jax.nn.silu(both[:, 0]) * both[:, 1]).astype(jnp.bfloat16)
    return jnp.dot(hidden, down, preferred_element_type=jnp.float32).astype(jnp.bfloat16)


def scatter_rows(normed_rows, slot_index, buffer_rows):
    slots = jnp.arange(buffer_rows, dtype=jnp.int32)
    select = jnp.sum(
        (slot_index[None, :, :] == slots[:, None, None]).astype(jnp.bfloat16), axis=-1
    )
    return jnp.dot(select, normed_rows, preferred_element_type=jnp.float32).astype(jnp.bfloat16)


def combine_rows(out_table, slot_index, gate_vals):
    slots = jnp.arange(out_table.shape[0], dtype=jnp.int32)
    weights = jnp.sum(
        jnp.where(slot_index[:, :, None] == slots[None, None, :], gate_vals[:, :, None], 0.0),
        axis=1,
    )
    high = weights.astype(jnp.bfloat16)
    low = (weights - high.astype(jnp.float32)).astype(jnp.bfloat16)
    return jnp.dot(high, out_table, preferred_element_type=jnp.float32) + jnp.dot(
        low, out_table, preferred_element_type=jnp.float32
    )


def seq_shift(x, shift, size):
    return lax.ppermute(x, "seq", [(i, (i + shift) % size) for i in range(size)])


def on_device(resid, qkv, w_out, norm_gain, router_w, expert_ids, w_gate_up, w_down):
    row_count = resid.shape[1]
    model_width = resid.shape[2]
    seq_size = lax.axis_size("seq")
    exp_size = lax.axis_size("exp")
    me = lax.axis_index("seq")
    seq_length = row_count * seq_size
    head_local = H // seq_size
    local_width = head_local * HD
    packed = qkv[0].reshape(row_count, 3, seq_size, local_width)
    pieces = []
    for shift in range(seq_size):
        target = (me + shift) % seq_size
        piece = lax.dynamic_index_in_dim(packed, target, axis=2, keepdims=False)
        pieces.append(piece if shift == 0 else seq_shift(piece, shift, seq_size))
    regrouped = jnp.stack(pieces, axis=0).reshape(seq_length, 3, local_width)
    queries = regrouped[:, 0].reshape(seq_length, head_local, HD)
    keys_all = regrouped[:, 1].reshape(seq_length, head_local, HD)
    values_all = regrouped[:, 2].reshape(seq_length, head_local, HD)
    scores = jnp.einsum(
        "qhd,khd->hqk", queries, keys_all, preferred_element_type=jnp.float32
    ) / math.sqrt(HD)
    weights = jax.nn.softmax(scores, axis=-1).astype(jnp.bfloat16)
    attended = jnp.einsum(
        "hqk,khd->qhd", weights, values_all, preferred_element_type=jnp.float32
    ).reshape(seq_length, local_width).astype(jnp.bfloat16)
    partial = jnp.dot(attended, w_out, preferred_element_type=jnp.float32).reshape(
        seq_size, row_count, model_width
    )
    projected = partial[0]
    for shift in range(1, seq_size):
        projected = projected + seq_shift(partial[shift], -shift, seq_size)
    mixed = resid[0].astype(jnp.float32) + projected
    meansq = jnp.mean(mixed * mixed, axis=-1, keepdims=True)
    normed = (mixed * lax.rsqrt(meansq + epsilon) * norm_gain).astype(jnp.bfloat16)
    exp_local = w_gate_up.shape[0]
    slot_cap = row_count // 8
    gathered = jnp.concatenate(
        [normed] + [seq_shift(normed, shift, seq_size) for shift in range(1, seq_size)], axis=0
    ).reshape(seq_size, row_count, model_width)
    far = seq_size // 2
    blocks_abs = (me - jnp.arange(seq_size, dtype=jnp.int32)) % seq_size
    chosen_all = jnp.take(expert_ids[0].reshape(seq_size, row_count, -1), blocks_abs, axis=0)
    direct_rows = jnp.concatenate([gathered[0], gathered[far]], axis=0)
    chosen = jnp.concatenate([chosen_all[0], chosen_all[far]], axis=0)
    gate_vals = gate_weights(direct_rows, router_w, chosen)
    ranks = slot_ranks(chosen, row_count, EXPERTS)
    kind = (jnp.arange(2 * row_count, dtype=jnp.int32) // row_count)[:, None]
    slot_index = chosen * (2 * slot_cap) + kind * slot_cap + ranks
    outgoing = scatter_rows(direct_rows, slot_index, EXPERTS * 2 * slot_cap)
    outgoing = outgoing.reshape(exp_size, exp_local, 2, slot_cap, model_width)
    homes = []
    for local in range(exp_local):
        received = lax.all_to_all(
            outgoing[:, local], "exp", split_axis=0, concat_axis=0, tiled=True
        )
        own_rows = received[:, 0]
        left_rows = seq_shift(own_rows, 1, seq_size)
        right_rows = seq_shift(own_rows, -1, seq_size)
        rows_in = jnp.stack([own_rows, received[:, 1], left_rows, right_rows], axis=0)
        parts = expert_one(
            rows_in.reshape(-1, model_width), w_gate_up[local], w_down[local]
        ).reshape(rows_in.shape)
        from_right = seq_shift(parts[2], -1, seq_size)
        from_left = seq_shift(parts[3], 1, seq_size)
        own_sum = (
            parts[0].astype(jnp.float32)
            + from_right.astype(jnp.float32)
            + from_left.astype(jnp.float32)
        ).astype(jnp.bfloat16)
        back = jnp.stack([own_sum, parts[1]], axis=1)
        homes.append(lax.all_to_all(back, "exp", split_axis=0, concat_axis=0, tiled=True))
    out_table = jnp.stack(homes, axis=1).reshape(-1, model_width)
    combined = combine_rows(out_table, slot_index, gate_vals)
    far_part = seq_shift(combined[row_count:].astype(jnp.bfloat16), far, seq_size)
    expert_sum = combined[:row_count] + far_part.astype(jnp.float32)
    return (mixed + expert_sum).astype(jnp.bfloat16).reshape(1, row_count, model_width)


def solution(mesh):
    in_specs = (
        P("exp", "seq", None),
        P("exp", "seq", None),
        P("seq", None),
        P(),
        P(),
        P("exp", None, None),
        P("exp", None, None, "seq"),
        P("exp", "seq", None),
    )
    out_specs = P("exp", "seq", None)
    return jax.shard_map(
        on_device, mesh=mesh, in_specs=in_specs, out_specs=out_specs, check_vma=False
    )
```

```python
import math

import jax
import jax.numpy as jnp
from jax import lax
from jax.sharding import PartitionSpec as P

H = 16
HD = 128
EXPERTS = 64


epsilon = 1e-05


def gate_weights(normed_rows, router_w, chosen):
    logits = jnp.dot(normed_rows, router_w, preferred_element_type=jnp.float32)
    match = chosen[:, :, None] == jnp.arange(logits.shape[1], dtype=jnp.int32)[None, None, :]
    picked = jnp.sum(jnp.where(match, logits[:, None, :], jnp.zeros((), logits.dtype)), axis=-1)
    squashed = jax.nn.sigmoid(picked)
    return squashed / jnp.sum(squashed, axis=-1, keepdims=True)


def slot_ranks(chosen, block_rows, experts):
    blocks = chosen.shape[0] // block_rows
    width = block_rows * chosen.shape[1]
    grouped = chosen.reshape(blocks, width)
    hits = (grouped[:, :, None] == jnp.arange(experts, dtype=jnp.int32)[None, None, :]).astype(
        jnp.bfloat16
    )
    lower = jnp.arange(width)[:, None] >= jnp.arange(width)[None, :]
    counts = jnp.einsum(
        "ij,bje->bie", lower.astype(jnp.bfloat16), hits, preferred_element_type=jnp.float32
    )
    ranks = jnp.sum(counts * hits.astype(jnp.float32), axis=-1) - 1
    return ranks.astype(jnp.int32).reshape(chosen.shape)


def expert_group(rows, gate_up, down):
    both = jnp.einsum("gsd,dxf->gsxf", rows, gate_up, preferred_element_type=jnp.float32)
    hidden = (jax.nn.silu(both[..., 0, :]) * both[..., 1, :]).astype(jnp.bfloat16)
    return jnp.einsum("gsf,fd->gsd", hidden, down, preferred_element_type=jnp.float32).astype(
        jnp.bfloat16
    )


def scatter_rows(normed_rows, slot_index, buffer_rows):
    slots = jnp.arange(buffer_rows, dtype=jnp.int32)
    select = jnp.sum(
        (slot_index[None, :, :] == slots[:, None, None]).astype(jnp.bfloat16), axis=-1
    )
    return jnp.dot(select, normed_rows, preferred_element_type=jnp.float32).astype(jnp.bfloat16)


def combine_rows(out_table, slot_index, gate_vals):
    slots = jnp.arange(out_table.shape[0], dtype=jnp.int32)
    weights = jnp.sum(
        jnp.where(slot_index[:, :, None] == slots[None, None, :], gate_vals[:, :, None], 0.0),
        axis=1,
    )
    high = weights.astype(jnp.bfloat16)
    low = (weights - high.astype(jnp.float32)).astype(jnp.bfloat16)
    return jnp.dot(high, out_table, preferred_element_type=jnp.float32) + jnp.dot(
        low, out_table, preferred_element_type=jnp.float32
    )


def seq_shift(x, shift, size):
    return lax.ppermute(x, "seq", [(i, (i + shift) % size) for i in range(size)])


def on_device(resid, qkv, w_out, norm_gain, router_w, expert_ids, w_gate_up, w_down):
    row_count = resid.shape[1]
    model_width = resid.shape[2]
    seq_size = lax.axis_size("seq")
    exp_size = lax.axis_size("exp")
    me = lax.axis_index("seq")
    seq_length = row_count * seq_size
    head_local = H // seq_size
    local_width = head_local * HD
    packed = qkv[0].reshape(row_count, 3, seq_size, local_width)
    pieces = []
    for shift in range(seq_size):
        target = (me + shift) % seq_size
        piece = lax.dynamic_index_in_dim(packed, target, axis=2, keepdims=False)
        pieces.append(piece if shift == 0 else seq_shift(piece, shift, seq_size))
    regrouped = jnp.stack(pieces, axis=0).reshape(seq_length, 3, local_width)
    queries = regrouped[:, 0].reshape(seq_length, head_local, HD)
    keys_all = regrouped[:, 1].reshape(seq_length, head_local, HD)
    values_all = regrouped[:, 2].reshape(seq_length, head_local, HD)
    scores = jnp.einsum(
        "qhd,khd->hqk", queries, keys_all, preferred_element_type=jnp.float32
    ) / math.sqrt(HD)
    weights = jax.nn.softmax(scores, axis=-1).astype(jnp.bfloat16)
    attended = jnp.einsum(
        "hqk,khd->qhd", weights, values_all, preferred_element_type=jnp.float32
    ).reshape(seq_length, local_width).astype(jnp.bfloat16)
    partial = jnp.dot(attended, w_out, preferred_element_type=jnp.float32).reshape(
        seq_size, row_count, model_width
    )
    projected = partial[0]
    for shift in range(1, seq_size):
        projected = projected + seq_shift(partial[shift], -shift, seq_size)
    mixed = resid[0].astype(jnp.float32) + projected
    meansq = jnp.mean(mixed * mixed, axis=-1, keepdims=True)
    normed = (mixed * lax.rsqrt(meansq + epsilon) * norm_gain).astype(jnp.bfloat16)
    exp_local = w_gate_up.shape[0]
    slot_cap = row_count // 8
    gathered = jnp.concatenate(
        [normed] + [seq_shift(normed, shift, seq_size) for shift in range(1, seq_size)], axis=0
    ).reshape(seq_size, row_count, model_width)
    far = seq_size // 2
    blocks_abs = (me - jnp.arange(seq_size, dtype=jnp.int32)) % seq_size
    chosen_all = jnp.take(expert_ids[0].reshape(seq_size, row_count, -1), blocks_abs, axis=0)
    direct_rows = jnp.concatenate([gathered[0], gathered[far]], axis=0)
    chosen = jnp.concatenate([chosen_all[0], chosen_all[far]], axis=0)
    gate_vals = gate_weights(direct_rows, router_w, chosen)
    ranks = slot_ranks(chosen, row_count, EXPERTS)
    kind = (jnp.arange(2 * row_count, dtype=jnp.int32) // row_count)[:, None]
    owner = chosen // exp_local
    local_of = chosen % exp_local
    slot_index = ((local_of * exp_size + owner) * 2 + kind) * slot_cap + ranks
    grid = (exp_local, exp_size, 2 * slot_cap)
    slot_ids = jnp.arange(math.prod(grid), dtype=jnp.int32).reshape(grid)
    select = jnp.sum(
        (slot_index[None, None, None, :, :] == slot_ids[..., None, None]).astype(
            jnp.bfloat16
        ),
        axis=-1,
    )
    outgoing = jnp.einsum(
        "cgsp,pd->cgsd", select, direct_rows, preferred_element_type=jnp.float32
    ).astype(jnp.bfloat16)
    homes = []
    for local in range(exp_local):
        direction = 1 if local % 2 == 0 else -1
        received = lax.all_to_all(outgoing[local], "exp", split_axis=0, concat_axis=0, tiled=True)
        forwarded = seq_shift(received, direction, seq_size)
        mine = expert_group(received, w_gate_up[local], w_down[local])
        theirs = expert_group(forwarded, w_gate_up[local], w_down[local])
        returned = seq_shift(theirs, -direction, seq_size)
        pair_sum = (mine.astype(jnp.float32) + returned.astype(jnp.float32)).astype(jnp.bfloat16)
        homes.append(lax.all_to_all(pair_sum, "exp", split_axis=0, concat_axis=0, tiled=True))
    table = jnp.stack(homes, axis=0)
    weights = jnp.sum(
        jnp.where(
            slot_index[:, :, None, None, None] == slot_ids[None, None],
            gate_vals[:, :, None, None, None],
            0.0,
        ),
        axis=1,
    )
    high = weights.astype(jnp.bfloat16)
    low = (weights - high.astype(jnp.float32)).astype(jnp.bfloat16)
    combined = jnp.einsum(
        "pcgs,cgsd->pd", high, table, preferred_element_type=jnp.float32
    ) + jnp.einsum("pcgs,cgsd->pd", low, table, preferred_element_type=jnp.float32)
    far_part = seq_shift(combined[row_count:].astype(jnp.bfloat16), far, seq_size)
    expert_sum = combined[:row_count] + far_part.astype(jnp.float32)
    return (mixed + expert_sum).astype(jnp.bfloat16).reshape(1, row_count, model_width)


def solution(mesh):
    in_specs = (
        P("exp", "seq", None),
        P("exp", "seq", None),
        P("seq", None),
        P(),
        P(),
        P("exp", None, None),
        P("exp", None, None, "seq"),
        P("exp", "seq", None),
    )
    out_specs = P("exp", "seq", None)
    return jax.shard_map(
        on_device, mesh=mesh, in_specs=in_specs, out_specs=out_specs, check_vma=False
    )
```

```python
import math

import jax
import jax.numpy as jnp
from jax import lax
from jax.sharding import PartitionSpec as P

H = 16
HD = 128
EXPERTS = 64


epsilon = 1e-05


def gate_weights(normed_rows, router_w, chosen):
    logits = jnp.dot(normed_rows, router_w, preferred_element_type=jnp.float32)
    match = chosen[:, :, None] == jnp.arange(logits.shape[1], dtype=jnp.int32)[None, None, :]
    picked = jnp.sum(jnp.where(match, logits[:, None, :], jnp.zeros((), logits.dtype)), axis=-1)
    squashed = jax.nn.sigmoid(picked)
    return squashed / jnp.sum(squashed, axis=-1, keepdims=True)


def slot_ranks(chosen, block_rows, experts):
    blocks = chosen.shape[0] // block_rows
    width = block_rows * chosen.shape[1]
    grouped = chosen.reshape(blocks, width)
    hits = (grouped[:, :, None] == jnp.arange(experts, dtype=jnp.int32)[None, None, :]).astype(
        jnp.bfloat16
    )
    lower = jnp.arange(width)[:, None] >= jnp.arange(width)[None, :]
    counts = jnp.einsum(
        "ij,bje->bie", lower.astype(jnp.bfloat16), hits, preferred_element_type=jnp.float32
    )
    ranks = jnp.sum(counts * hits.astype(jnp.float32), axis=-1) - 1
    return ranks.astype(jnp.int32).reshape(chosen.shape)


def expert_group(rows, gate_up, down):
    both = jnp.einsum("gsd,dxf->gsxf", rows, gate_up, preferred_element_type=jnp.float32)
    hidden = (jax.nn.silu(both[..., 0, :]) * both[..., 1, :]).astype(jnp.bfloat16)
    return jnp.einsum("gsf,fd->gsd", hidden, down, preferred_element_type=jnp.float32).astype(
        jnp.bfloat16
    )


def scatter_rows(normed_rows, slot_index, buffer_rows):
    slots = jnp.arange(buffer_rows, dtype=jnp.int32)
    select = jnp.sum(
        (slot_index[None, :, :] == slots[:, None, None]).astype(jnp.bfloat16), axis=-1
    )
    return jnp.dot(select, normed_rows, preferred_element_type=jnp.float32).astype(jnp.bfloat16)


def combine_rows(out_table, slot_index, gate_vals):
    slots = jnp.arange(out_table.shape[0], dtype=jnp.int32)
    weights = jnp.sum(
        jnp.where(slot_index[:, :, None] == slots[None, None, :], gate_vals[:, :, None], 0.0),
        axis=1,
    )
    high = weights.astype(jnp.bfloat16)
    low = (weights - high.astype(jnp.float32)).astype(jnp.bfloat16)
    return jnp.dot(high, out_table, preferred_element_type=jnp.float32) + jnp.dot(
        low, out_table, preferred_element_type=jnp.float32
    )


def seq_shift(x, shift, size):
    return lax.ppermute(x, "seq", [(i, (i + shift) % size) for i in range(size)])


def paired_shift(x, local, seq_size, exp_size, back):
    pairs = []
    for s in range(seq_size):
        for e in range(exp_size):
            step = 1 if (local + e) % 2 == 0 else -1
            if back:
                step = -step
            pairs.append((s * exp_size + e, ((s + step) % seq_size) * exp_size + e))
    return lax.ppermute(x, ("seq", "exp"), pairs)


def on_device(resid, qkv, w_out, norm_gain, router_w, expert_ids, w_gate_up, w_down):
    row_count = resid.shape[1]
    model_width = resid.shape[2]
    seq_size = lax.axis_size("seq")
    exp_size = lax.axis_size("exp")
    me = lax.axis_index("seq")
    seq_length = row_count * seq_size
    head_local = H // seq_size
    local_width = head_local * HD
    packed = qkv[0].reshape(row_count, 3, seq_size, local_width)
    pieces = []
    for shift in range(seq_size):
        target = (me + shift) % seq_size
        piece = lax.dynamic_index_in_dim(packed, target, axis=2, keepdims=False)
        pieces.append(piece if shift == 0 else seq_shift(piece, shift, seq_size))
    regrouped = jnp.stack(pieces, axis=0).reshape(seq_length, 3, local_width)
    queries = regrouped[:, 0].reshape(seq_length, head_local, HD)
    keys_all = regrouped[:, 1].reshape(seq_length, head_local, HD)
    values_all = regrouped[:, 2].reshape(seq_length, head_local, HD)
    scores = jnp.einsum(
        "qhd,khd->hqk", queries, keys_all, preferred_element_type=jnp.float32
    ) / math.sqrt(HD)
    weights = jax.nn.softmax(scores, axis=-1).astype(jnp.bfloat16)
    attended = jnp.einsum(
        "hqk,khd->qhd", weights, values_all, preferred_element_type=jnp.float32
    ).reshape(seq_length, local_width).astype(jnp.bfloat16)
    partial = jnp.dot(attended, w_out, preferred_element_type=jnp.float32).reshape(
        seq_size, row_count, model_width
    )
    projected = partial[0]
    for shift in range(1, seq_size):
        projected = projected + seq_shift(partial[shift], -shift, seq_size)
    mixed = resid[0].astype(jnp.float32) + projected
    meansq = jnp.mean(mixed * mixed, axis=-1, keepdims=True)
    normed = (mixed * lax.rsqrt(meansq + epsilon) * norm_gain).astype(jnp.bfloat16)
    exp_local = w_gate_up.shape[0]
    slot_cap = row_count // 8
    gathered = jnp.concatenate(
        [normed] + [seq_shift(normed, shift, seq_size) for shift in range(1, seq_size)], axis=0
    ).reshape(seq_size, row_count, model_width)
    far = seq_size // 2
    blocks_abs = (me - jnp.arange(seq_size, dtype=jnp.int32)) % seq_size
    chosen_all = jnp.take(expert_ids[0].reshape(seq_size, row_count, -1), blocks_abs, axis=0)
    direct_rows = jnp.concatenate([gathered[0], gathered[far]], axis=0)
    chosen = jnp.concatenate([chosen_all[0], chosen_all[far]], axis=0)
    gate_vals = gate_weights(direct_rows, router_w, chosen)
    ranks = slot_ranks(chosen, row_count, EXPERTS)
    kind = (jnp.arange(2 * row_count, dtype=jnp.int32) // row_count)[:, None]
    owner = chosen // exp_local
    local_of = chosen % exp_local
    slot_index = ((local_of * exp_size + owner) * 2 + kind) * slot_cap + ranks
    grid = (exp_local, exp_size, 2 * slot_cap)
    slot_ids = jnp.arange(math.prod(grid), dtype=jnp.int32).reshape(grid)
    select = jnp.sum(
        (slot_index[None, None, None, :, :] == slot_ids[..., None, None]).astype(
            jnp.bfloat16
        ),
        axis=-1,
    )
    outgoing = jnp.einsum(
        "cgsp,pd->cgsd", select, direct_rows, preferred_element_type=jnp.float32
    ).astype(jnp.bfloat16)
    homes = []
    for local in range(exp_local):
        received = lax.all_to_all(outgoing[local], "exp", split_axis=0, concat_axis=0, tiled=True)
        forwarded = paired_shift(received, local, seq_size, exp_size, False)
        mine = expert_group(received, w_gate_up[local], w_down[local])
        theirs = expert_group(forwarded, w_gate_up[local], w_down[local])
        returned = paired_shift(theirs, local, seq_size, exp_size, True)
        pair_sum = (mine.astype(jnp.float32) + returned.astype(jnp.float32)).astype(jnp.bfloat16)
        homes.append(lax.all_to_all(pair_sum, "exp", split_axis=0, concat_axis=0, tiled=True))
    table = jnp.stack(homes, axis=0)
    weights = jnp.sum(
        jnp.where(
            slot_index[:, :, None, None, None] == slot_ids[None, None],
            gate_vals[:, :, None, None, None],
            0.0,
        ),
        axis=1,
    )
    high = weights.astype(jnp.bfloat16)
    low = (weights - high.astype(jnp.float32)).astype(jnp.bfloat16)
    combined = jnp.einsum(
        "pcgs,cgsd->pd", high, table, preferred_element_type=jnp.float32
    ) + jnp.einsum("pcgs,cgsd->pd", low, table, preferred_element_type=jnp.float32)
    far_part = seq_shift(combined[row_count:].astype(jnp.bfloat16), far, seq_size)
    expert_sum = combined[:row_count] + far_part.astype(jnp.float32)
    return (mixed + expert_sum).astype(jnp.bfloat16).reshape(1, row_count, model_width)


def solution(mesh):
    in_specs = (
        P("exp", "seq", None),
        P("exp", "seq", None),
        P("seq", None),
        P(),
        P(),
        P("exp", None, None),
        P("exp", None, None, "seq"),
        P("exp", "seq", None),
    )
    out_specs = P("exp", "seq", None)
    return jax.shard_map(
        on_device, mesh=mesh, in_specs=in_specs, out_specs=out_specs, check_vma=False
    )
```

```python
import math

import jax
import jax.numpy as jnp
from jax import lax
from jax.sharding import PartitionSpec as P

H = 16
HD = 128
EXPERTS = 64


epsilon = 1e-05


def gate_weights(normed_rows, router_w, chosen):
    logits = jnp.dot(normed_rows, router_w, preferred_element_type=jnp.float32)
    match = chosen[:, :, None] == jnp.arange(logits.shape[1], dtype=jnp.int32)[None, None, :]
    picked = jnp.sum(jnp.where(match, logits[:, None, :], jnp.zeros((), logits.dtype)), axis=-1)
    squashed = jax.nn.sigmoid(picked)
    return squashed / jnp.sum(squashed, axis=-1, keepdims=True)


def slot_ranks(chosen, block_rows, experts):
    blocks = chosen.shape[0] // block_rows
    width = block_rows * chosen.shape[1]
    grouped = chosen.reshape(blocks, width)
    hits = (grouped[:, :, None] == jnp.arange(experts, dtype=jnp.int32)[None, None, :]).astype(
        jnp.bfloat16
    )
    lower = jnp.arange(width)[:, None] >= jnp.arange(width)[None, :]
    counts = jnp.einsum(
        "ij,bje->bie", lower.astype(jnp.bfloat16), hits, preferred_element_type=jnp.float32
    )
    ranks = jnp.sum(counts * hits.astype(jnp.float32), axis=-1) - 1
    return ranks.astype(jnp.int32).reshape(chosen.shape)


def expert_group(rows, gate_up, down):
    both = jnp.einsum("gsd,dxf->gsxf", rows, gate_up, preferred_element_type=jnp.float32)
    hidden = (jax.nn.silu(both[..., 0, :]) * both[..., 1, :]).astype(jnp.bfloat16)
    return jnp.einsum("gsf,fd->gsd", hidden, down, preferred_element_type=jnp.float32).astype(
        jnp.bfloat16
    )


def scatter_rows(normed_rows, slot_index, buffer_rows):
    slots = jnp.arange(buffer_rows, dtype=jnp.int32)
    select = jnp.sum(
        (slot_index[None, :, :] == slots[:, None, None]).astype(jnp.bfloat16), axis=-1
    )
    return jnp.dot(select, normed_rows, preferred_element_type=jnp.float32).astype(jnp.bfloat16)


def combine_rows(out_table, slot_index, gate_vals):
    slots = jnp.arange(out_table.shape[0], dtype=jnp.int32)
    weights = jnp.sum(
        jnp.where(slot_index[:, :, None] == slots[None, None, :], gate_vals[:, :, None], 0.0),
        axis=1,
    )
    high = weights.astype(jnp.bfloat16)
    low = (weights - high.astype(jnp.float32)).astype(jnp.bfloat16)
    return jnp.dot(high, out_table, preferred_element_type=jnp.float32) + jnp.dot(
        low, out_table, preferred_element_type=jnp.float32
    )


def seq_shift(x, shift, size):
    return lax.ppermute(x, "seq", [(i, (i + shift) % size) for i in range(size)])


def paired_shift(x, local, seq_size, exp_size, back):
    pairs = []
    for s in range(seq_size):
        for e in range(exp_size):
            step = 1 if e % 2 == 0 else -1
            if back:
                step = -step
            pairs.append((s * exp_size + e, ((s + step) % seq_size) * exp_size + e))
    return lax.ppermute(x, ("seq", "exp"), pairs)


def on_device(resid, qkv, w_out, norm_gain, router_w, expert_ids, w_gate_up, w_down):
    row_count = resid.shape[1]
    model_width = resid.shape[2]
    seq_size = lax.axis_size("seq")
    exp_size = lax.axis_size("exp")
    me = lax.axis_index("seq")
    seq_length = row_count * seq_size
    head_local = H // seq_size
    local_width = head_local * HD
    packed = qkv[0].reshape(row_count, 3, seq_size, local_width)
    pieces = []
    for shift in range(seq_size):
        target = (me + shift) % seq_size
        piece = lax.dynamic_index_in_dim(packed, target, axis=2, keepdims=False)
        pieces.append(piece if shift == 0 else seq_shift(piece, shift, seq_size))
    regrouped = jnp.stack(pieces, axis=0).reshape(seq_length, 3, local_width)
    queries = regrouped[:, 0].reshape(seq_length, head_local, HD)
    keys_all = regrouped[:, 1].reshape(seq_length, head_local, HD)
    values_all = regrouped[:, 2].reshape(seq_length, head_local, HD)
    scores = jnp.einsum(
        "qhd,khd->hqk", queries, keys_all, preferred_element_type=jnp.float32
    ) / math.sqrt(HD)
    weights = jax.nn.softmax(scores, axis=-1).astype(jnp.bfloat16)
    attended = jnp.einsum(
        "hqk,khd->qhd", weights, values_all, preferred_element_type=jnp.float32
    ).reshape(seq_length, local_width).astype(jnp.bfloat16)
    partial = jnp.dot(attended, w_out, preferred_element_type=jnp.float32).reshape(
        seq_size, row_count, model_width
    )
    projected = partial[0]
    for shift in range(1, seq_size):
        projected = projected + seq_shift(partial[shift], -shift, seq_size)
    mixed = resid[0].astype(jnp.float32) + projected
    meansq = jnp.mean(mixed * mixed, axis=-1, keepdims=True)
    normed = (mixed * lax.rsqrt(meansq + epsilon) * norm_gain).astype(jnp.bfloat16)
    exp_local = w_gate_up.shape[0]
    slot_cap = row_count // 8
    gathered = jnp.concatenate(
        [normed] + [seq_shift(normed, shift, seq_size) for shift in range(1, seq_size)], axis=0
    ).reshape(seq_size, row_count, model_width)
    far = seq_size // 2
    blocks_abs = (me - jnp.arange(seq_size, dtype=jnp.int32)) % seq_size
    chosen_all = jnp.take(expert_ids[0].reshape(seq_size, row_count, -1), blocks_abs, axis=0)
    direct_rows = jnp.concatenate([gathered[0], gathered[far]], axis=0)
    chosen = jnp.concatenate([chosen_all[0], chosen_all[far]], axis=0)
    gate_vals = gate_weights(direct_rows, router_w, chosen)
    ranks = slot_ranks(chosen, row_count, EXPERTS)
    kind = (jnp.arange(2 * row_count, dtype=jnp.int32) // row_count)[:, None]
    owner = chosen // exp_local
    local_of = chosen % exp_local
    slot_index = ((local_of * exp_size + owner) * 2 + kind) * slot_cap + ranks
    grid = (exp_local, exp_size, 2 * slot_cap)
    slot_ids = jnp.arange(math.prod(grid), dtype=jnp.int32).reshape(grid)
    select = jnp.sum(
        (slot_index[None, None, None, :, :] == slot_ids[..., None, None]).astype(
            jnp.bfloat16
        ),
        axis=-1,
    )
    outgoing = jnp.einsum(
        "cgsp,pd->cgsd", select, direct_rows, preferred_element_type=jnp.float32
    ).astype(jnp.bfloat16)
    homes = []
    for local in range(exp_local):
        received = lax.all_to_all(outgoing[local], "exp", split_axis=0, concat_axis=0, tiled=True)
        forwarded = paired_shift(received, local, seq_size, exp_size, False)
        mine = expert_group(received, w_gate_up[local], w_down[local])
        theirs = expert_group(forwarded, w_gate_up[local], w_down[local])
        returned = paired_shift(theirs, local, seq_size, exp_size, True)
        pair_sum = (mine.astype(jnp.float32) + returned.astype(jnp.float32)).astype(jnp.bfloat16)
        homes.append(lax.all_to_all(pair_sum, "exp", split_axis=0, concat_axis=0, tiled=True))
    table = jnp.stack(homes, axis=0)
    weights = jnp.sum(
        jnp.where(
            slot_index[:, :, None, None, None] == slot_ids[None, None],
            gate_vals[:, :, None, None, None],
            0.0,
        ),
        axis=1,
    )
    high = weights.astype(jnp.bfloat16)
    low = (weights - high.astype(jnp.float32)).astype(jnp.bfloat16)
    combined = jnp.einsum(
        "pcgs,cgsd->pd", high, table, preferred_element_type=jnp.float32
    ) + jnp.einsum("pcgs,cgsd->pd", low, table, preferred_element_type=jnp.float32)
    far_part = seq_shift(combined[row_count:].astype(jnp.bfloat16), far, seq_size)
    expert_sum = combined[:row_count] + far_part.astype(jnp.float32)
    return (mixed + expert_sum).astype(jnp.bfloat16).reshape(1, row_count, model_width)


def solution(mesh):
    in_specs = (
        P("exp", "seq", None),
        P("exp", "seq", None),
        P("seq", None),
        P(),
        P(),
        P("exp", None, None),
        P("exp", None, None, "seq"),
        P("exp", "seq", None),
    )
    out_specs = P("exp", "seq", None)
    return jax.shard_map(
        on_device, mesh=mesh, in_specs=in_specs, out_specs=out_specs, check_vma=False
    )
```

```python
import math

import jax
import jax.numpy as jnp
from jax import lax
from jax.sharding import PartitionSpec as P

H = 16
HD = 128
EXPERTS = 64


epsilon = 1e-05


def gate_weights(normed_rows, router_w, chosen):
    logits = jnp.dot(normed_rows, router_w, preferred_element_type=jnp.float32)
    match = chosen[:, :, None] == jnp.arange(logits.shape[1], dtype=jnp.int32)[None, None, :]
    picked = jnp.sum(jnp.where(match, logits[:, None, :], jnp.zeros((), logits.dtype)), axis=-1)
    squashed = jax.nn.sigmoid(picked)
    return squashed / jnp.sum(squashed, axis=-1, keepdims=True)


def slot_ranks(chosen, block_rows, experts):
    blocks = chosen.shape[0] // block_rows
    width = block_rows * chosen.shape[1]
    grouped = chosen.reshape(blocks, width)
    hits = (grouped[:, :, None] == jnp.arange(experts, dtype=jnp.int32)[None, None, :]).astype(
        jnp.bfloat16
    )
    lower = jnp.arange(width)[:, None] >= jnp.arange(width)[None, :]
    counts = jnp.einsum(
        "ij,bje->bie", lower.astype(jnp.bfloat16), hits, preferred_element_type=jnp.float32
    )
    ranks = jnp.sum(counts * hits.astype(jnp.float32), axis=-1) - 1
    return ranks.astype(jnp.int32).reshape(chosen.shape)


def expert_group(rows, gate_up, down):
    both = jnp.einsum("gsd,dxf->gsxf", rows, gate_up, preferred_element_type=jnp.float32)
    hidden = (jax.nn.silu(both[..., 0, :]) * both[..., 1, :]).astype(jnp.bfloat16)
    return jnp.einsum("gsf,fd->gsd", hidden, down, preferred_element_type=jnp.float32).astype(
        jnp.bfloat16
    )


def expert_halves(rows, gate_up, down):
    both = sum(
        jnp.einsum("gsd,dxf->gsxf", rows[h], gate_up[h], preferred_element_type=jnp.float32)
        for h in range(len(rows))
    )
    hidden = (jax.nn.silu(both[..., 0, :]) * both[..., 1, :]).astype(jnp.bfloat16)
    return [
        jnp.einsum("gsf,fd->gsd", hidden, down[:, h], preferred_element_type=jnp.float32).astype(
            jnp.bfloat16
        )
        for h in range(len(rows))
    ]


def scatter_rows(normed_rows, slot_index, buffer_rows):
    slots = jnp.arange(buffer_rows, dtype=jnp.int32)
    select = jnp.sum(
        (slot_index[None, :, :] == slots[:, None, None]).astype(jnp.bfloat16), axis=-1
    )
    return jnp.dot(select, normed_rows, preferred_element_type=jnp.float32).astype(jnp.bfloat16)


def combine_rows(out_table, slot_index, gate_vals):
    slots = jnp.arange(out_table.shape[0], dtype=jnp.int32)
    weights = jnp.sum(
        jnp.where(slot_index[:, :, None] == slots[None, None, :], gate_vals[:, :, None], 0.0),
        axis=1,
    )
    high = weights.astype(jnp.bfloat16)
    low = (weights - high.astype(jnp.float32)).astype(jnp.bfloat16)
    return jnp.dot(high, out_table, preferred_element_type=jnp.float32) + jnp.dot(
        low, out_table, preferred_element_type=jnp.float32
    )


def seq_shift(x, shift, size):
    return lax.ppermute(x, "seq", [(i, (i + shift) % size) for i in range(size)])


def paired_shift(x, local, seq_size, exp_size, back):
    pairs = []
    for s in range(seq_size):
        for e in range(exp_size):
            step = 1 if e % 2 == 0 else -1
            if back:
                step = -step
            pairs.append((s * exp_size + e, ((s + step) % seq_size) * exp_size + e))
    return lax.ppermute(x, ("seq", "exp"), pairs)


def on_device(resid, qkv, w_out, norm_gain, router_w, expert_ids, w_gate_up, w_down):
    row_count = resid.shape[1]
    model_width = resid.shape[2]
    seq_size = lax.axis_size("seq")
    exp_size = lax.axis_size("exp")
    me = lax.axis_index("seq")
    seq_length = row_count * seq_size
    head_local = H // seq_size
    local_width = head_local * HD
    packed = qkv[0].reshape(row_count, 3, seq_size, local_width)
    pieces = []
    for shift in range(seq_size):
        target = (me + shift) % seq_size
        piece = lax.dynamic_index_in_dim(packed, target, axis=2, keepdims=False)
        pieces.append(piece if shift == 0 else seq_shift(piece, shift, seq_size))
    regrouped = jnp.stack(pieces, axis=0).reshape(seq_length, 3, local_width)
    queries = regrouped[:, 0].reshape(seq_length, head_local, HD)
    keys_all = regrouped[:, 1].reshape(seq_length, head_local, HD)
    values_all = regrouped[:, 2].reshape(seq_length, head_local, HD)
    scores = jnp.einsum(
        "qhd,khd->hqk", queries, keys_all, preferred_element_type=jnp.float32
    ) / math.sqrt(HD)
    weights = jax.nn.softmax(scores, axis=-1).astype(jnp.bfloat16)
    attended = jnp.einsum(
        "hqk,khd->qhd", weights, values_all, preferred_element_type=jnp.float32
    ).reshape(seq_length, local_width).astype(jnp.bfloat16)
    partial = jnp.dot(attended, w_out, preferred_element_type=jnp.float32).reshape(
        seq_size, row_count, model_width
    )
    projected = partial[0]
    for shift in range(1, seq_size):
        projected = projected + seq_shift(partial[shift], -shift, seq_size)
    mixed = resid[0].astype(jnp.float32) + projected
    meansq = jnp.mean(mixed * mixed, axis=-1, keepdims=True)
    normed = (mixed * lax.rsqrt(meansq + epsilon) * norm_gain).astype(jnp.bfloat16)
    exp_local = w_gate_up.shape[0]
    slot_cap = row_count // 8
    gathered = jnp.concatenate(
        [normed] + [seq_shift(normed, shift, seq_size) for shift in range(1, seq_size)], axis=0
    ).reshape(seq_size, row_count, model_width)
    far = seq_size // 2
    blocks_abs = (me - jnp.arange(seq_size, dtype=jnp.int32)) % seq_size
    chosen_all = jnp.take(expert_ids[0].reshape(seq_size, row_count, -1), blocks_abs, axis=0)
    direct_rows = jnp.concatenate([gathered[0], gathered[far]], axis=0)
    chosen = jnp.concatenate([chosen_all[0], chosen_all[far]], axis=0)
    gate_vals = gate_weights(direct_rows, router_w, chosen)
    ranks = slot_ranks(chosen, row_count, EXPERTS)
    kind = (jnp.arange(2 * row_count, dtype=jnp.int32) // row_count)[:, None]
    owner = chosen // exp_local
    local_of = chosen % exp_local
    slot_index = ((local_of * exp_size + owner) * 2 + kind) * slot_cap + ranks
    grid = (exp_local, exp_size, 2 * slot_cap)
    slot_ids = jnp.arange(math.prod(grid), dtype=jnp.int32).reshape(grid)
    select = jnp.sum(
        (slot_index[None, None, None, :, :] == slot_ids[..., None, None]).astype(
            jnp.bfloat16
        ),
        axis=-1,
    )
    halves = 2
    half_width = model_width // halves
    outgoing = jnp.einsum(
        "cgsp,phd->chgsd",
        select,
        direct_rows.reshape(-1, halves, half_width),
        preferred_element_type=jnp.float32,
    ).astype(jnp.bfloat16)
    homes = []
    for local in range(exp_local):
        received = [
            lax.all_to_all(outgoing[local, h], "exp", split_axis=0, concat_axis=0, tiled=True)
            for h in range(halves)
        ]
        forwarded = [paired_shift(piece, local, seq_size, exp_size, False) for piece in received]
        gate_up = w_gate_up[local].reshape(halves, half_width, 2, -1)
        down = w_down[local].reshape(-1, halves, half_width)
        mine = expert_halves(received, gate_up, down)
        theirs = expert_halves(forwarded, gate_up, down)
        pieces = []
        for h in range(halves):
            returned = paired_shift(theirs[h], local, seq_size, exp_size, True)
            pair_sum = (mine[h].astype(jnp.float32) + returned.astype(jnp.float32)).astype(
                jnp.bfloat16
            )
            pieces.append(
                lax.all_to_all(pair_sum, "exp", split_axis=0, concat_axis=0, tiled=True)
            )
        homes.append(jnp.stack(pieces, axis=0))
    table = jnp.stack(homes, axis=0)
    weights = jnp.sum(
        jnp.where(
            slot_index[:, :, None, None, None] == slot_ids[None, None],
            gate_vals[:, :, None, None, None],
            0.0,
        ),
        axis=1,
    )
    high = weights.astype(jnp.bfloat16)
    low = (weights - high.astype(jnp.float32)).astype(jnp.bfloat16)
    combined = (
        jnp.einsum("pcgs,chgsd->phd", high, table, preferred_element_type=jnp.float32)
        + jnp.einsum("pcgs,chgsd->phd", low, table, preferred_element_type=jnp.float32)
    ).reshape(-1, model_width)
    far_part = seq_shift(combined[row_count:].astype(jnp.bfloat16), far, seq_size)
    expert_sum = combined[:row_count] + far_part.astype(jnp.float32)
    return (mixed + expert_sum).astype(jnp.bfloat16).reshape(1, row_count, model_width)


def solution(mesh):
    in_specs = (
        P("exp", "seq", None),
        P("exp", "seq", None),
        P("seq", None),
        P(),
        P(),
        P("exp", None, None),
        P("exp", None, None, "seq"),
        P("exp", "seq", None),
    )
    out_specs = P("exp", "seq", None)
    return jax.shard_map(
        on_device, mesh=mesh, in_specs=in_specs, out_specs=out_specs, check_vma=False
    )
```

```python
import math

import jax
import jax.numpy as jnp
from jax import lax
from jax.sharding import PartitionSpec as P

H = 16
HD = 128
EXPERTS = 64


epsilon = 1e-05


def gate_weights(normed_rows, router_w, chosen):
    logits = jnp.dot(normed_rows, router_w, preferred_element_type=jnp.float32)
    match = chosen[:, :, None] == jnp.arange(logits.shape[1], dtype=jnp.int32)[None, None, :]
    picked = jnp.sum(jnp.where(match, logits[:, None, :], jnp.zeros((), logits.dtype)), axis=-1)
    squashed = jax.nn.sigmoid(picked)
    return squashed / jnp.sum(squashed, axis=-1, keepdims=True)


def slot_ranks(chosen, block_rows, experts):
    blocks = chosen.shape[0] // block_rows
    width = block_rows * chosen.shape[1]
    grouped = chosen.reshape(blocks, width)
    hits = (grouped[:, :, None] == jnp.arange(experts, dtype=jnp.int32)[None, None, :]).astype(
        jnp.bfloat16
    )
    lower = jnp.arange(width)[:, None] >= jnp.arange(width)[None, :]
    counts = jnp.einsum(
        "ij,bje->bie", lower.astype(jnp.bfloat16), hits, preferred_element_type=jnp.float32
    )
    ranks = jnp.sum(counts * hits.astype(jnp.float32), axis=-1) - 1
    return ranks.astype(jnp.int32).reshape(chosen.shape)


def expert_group(rows, gate_up, down):
    both = jnp.einsum("gsd,dxf->gsxf", rows, gate_up, preferred_element_type=jnp.float32)
    hidden = (jax.nn.silu(both[..., 0, :]) * both[..., 1, :]).astype(jnp.bfloat16)
    return jnp.einsum("gsf,fd->gsd", hidden, down, preferred_element_type=jnp.float32).astype(
        jnp.bfloat16
    )


def scatter_rows(normed_rows, slot_index, buffer_rows):
    slots = jnp.arange(buffer_rows, dtype=jnp.int32)
    select = jnp.sum(
        (slot_index[None, :, :] == slots[:, None, None]).astype(jnp.bfloat16), axis=-1
    )
    return jnp.dot(select, normed_rows, preferred_element_type=jnp.float32).astype(jnp.bfloat16)


def combine_rows(out_table, slot_index, gate_vals):
    slots = jnp.arange(out_table.shape[0], dtype=jnp.int32)
    weights = jnp.sum(
        jnp.where(slot_index[:, :, None] == slots[None, None, :], gate_vals[:, :, None], 0.0),
        axis=1,
    )
    high = weights.astype(jnp.bfloat16)
    low = (weights - high.astype(jnp.float32)).astype(jnp.bfloat16)
    return jnp.dot(high, out_table, preferred_element_type=jnp.float32) + jnp.dot(
        low, out_table, preferred_element_type=jnp.float32
    )


def seq_shift(x, shift, size):
    return lax.ppermute(x, "seq", [(i, (i + shift) % size) for i in range(size)])


def paired_shift(x, local, seq_size, exp_size, back):
    pairs = []
    for s in range(seq_size):
        for e in range(exp_size):
            step = 1 if e % 2 == 0 else -1
            if back:
                step = -step
            pairs.append((s * exp_size + e, ((s + step) % seq_size) * exp_size + e))
    return lax.ppermute(x, ("seq", "exp"), pairs)


def on_device(resid, qkv, w_out, norm_gain, router_w, expert_ids, w_gate_up, w_down):
    row_count = resid.shape[1]
    model_width = resid.shape[2]
    seq_size = lax.axis_size("seq")
    exp_size = lax.axis_size("exp")
    me = lax.axis_index("seq")
    seq_length = row_count * seq_size
    head_local = H // seq_size
    local_width = head_local * HD
    packed = qkv[0].reshape(row_count, 3, seq_size, local_width)
    pieces = []
    for shift in range(seq_size):
        target = (me + shift) % seq_size
        piece = lax.dynamic_index_in_dim(packed, target, axis=2, keepdims=False)
        pieces.append(piece if shift == 0 else seq_shift(piece, shift, seq_size))
    regrouped = jnp.stack(pieces, axis=0).reshape(seq_length, 3, local_width)
    queries = regrouped[:, 0].reshape(seq_length, head_local, HD)
    keys_all = regrouped[:, 1].reshape(seq_length, head_local, HD)
    values_all = regrouped[:, 2].reshape(seq_length, head_local, HD)
    scores = jnp.einsum(
        "qhd,khd->hqk", queries, keys_all, preferred_element_type=jnp.float32
    ) / math.sqrt(HD)
    weights = jax.nn.softmax(scores, axis=-1).astype(jnp.bfloat16)
    attended = jnp.einsum(
        "hqk,khd->qhd", weights, values_all, preferred_element_type=jnp.float32
    ).reshape(seq_length, local_width).astype(jnp.bfloat16)
    partial = jnp.dot(attended, w_out, preferred_element_type=jnp.float32).reshape(
        seq_size, row_count, model_width
    )
    projected = partial[0]
    for shift in range(1, seq_size):
        projected = projected + seq_shift(
            partial[shift].astype(jnp.bfloat16), -shift, seq_size
        ).astype(jnp.float32)
    mixed = resid[0].astype(jnp.float32) + projected
    meansq = jnp.mean(mixed * mixed, axis=-1, keepdims=True)
    normed = (mixed * lax.rsqrt(meansq + epsilon) * norm_gain).astype(jnp.bfloat16)
    exp_local = w_gate_up.shape[0]
    slot_cap = row_count // 8
    gathered = jnp.concatenate(
        [normed] + [seq_shift(normed, shift, seq_size) for shift in range(1, seq_size)], axis=0
    ).reshape(seq_size, row_count, model_width)
    far = seq_size // 2
    blocks_abs = (me - jnp.arange(seq_size, dtype=jnp.int32)) % seq_size
    chosen_all = jnp.take(expert_ids[0].reshape(seq_size, row_count, -1), blocks_abs, axis=0)
    direct_rows = jnp.concatenate([gathered[0], gathered[far]], axis=0)
    chosen = jnp.concatenate([chosen_all[0], chosen_all[far]], axis=0)
    gate_vals = gate_weights(direct_rows, router_w, chosen)
    ranks = slot_ranks(chosen, row_count, EXPERTS)
    kind = (jnp.arange(2 * row_count, dtype=jnp.int32) // row_count)[:, None]
    owner = chosen // exp_local
    local_of = chosen % exp_local
    slot_index = ((local_of * exp_size + owner) * 2 + kind) * slot_cap + ranks
    grid = (exp_local, exp_size, 2 * slot_cap)
    slot_ids = jnp.arange(math.prod(grid), dtype=jnp.int32).reshape(grid)
    select = jnp.sum(
        (slot_index[None, None, None, :, :] == slot_ids[..., None, None]).astype(
            jnp.bfloat16
        ),
        axis=-1,
    )
    outgoing = jnp.einsum(
        "cgsp,pd->cgsd", select, direct_rows, preferred_element_type=jnp.float32
    ).astype(jnp.bfloat16)
    homes = []
    for local in range(exp_local):
        received = lax.all_to_all(outgoing[local], "exp", split_axis=0, concat_axis=0, tiled=True)
        forwarded = paired_shift(received, local, seq_size, exp_size, False)
        mine = expert_group(received, w_gate_up[local], w_down[local])
        theirs = expert_group(forwarded, w_gate_up[local], w_down[local])
        returned = paired_shift(theirs, local, seq_size, exp_size, True)
        pair_sum = (mine.astype(jnp.float32) + returned.astype(jnp.float32)).astype(jnp.bfloat16)
        homes.append(lax.all_to_all(pair_sum, "exp", split_axis=0, concat_axis=0, tiled=True))
    table = jnp.stack(homes, axis=0)
    weights = jnp.sum(
        jnp.where(
            slot_index[:, :, None, None, None] == slot_ids[None, None],
            gate_vals[:, :, None, None, None],
            0.0,
        ),
        axis=1,
    )
    high = weights.astype(jnp.bfloat16)
    low = (weights - high.astype(jnp.float32)).astype(jnp.bfloat16)
    combined = jnp.einsum(
        "pcgs,cgsd->pd", high, table, preferred_element_type=jnp.float32
    ) + jnp.einsum("pcgs,cgsd->pd", low, table, preferred_element_type=jnp.float32)
    far_part = seq_shift(combined[row_count:].astype(jnp.bfloat16), far, seq_size)
    expert_sum = combined[:row_count] + far_part.astype(jnp.float32)
    return (mixed + expert_sum).astype(jnp.bfloat16).reshape(1, row_count, model_width)


def solution(mesh):
    in_specs = (
        P("exp", "seq", None),
        P("exp", "seq", None),
        P("seq", None),
        P(),
        P(),
        P("exp", None, None),
        P("exp", None, None, "seq"),
        P("exp", "seq", None),
    )
    out_specs = P("exp", "seq", None)
    return jax.shard_map(
        on_device, mesh=mesh, in_specs=in_specs, out_specs=out_specs, check_vma=False
    )
```

```python
import math

import jax
import jax.numpy as jnp
from jax import lax
from jax.sharding import PartitionSpec as P

H = 16
HD = 128
EXPERTS = 64


epsilon = 1e-05


def gate_weights(normed_rows, router_w, chosen):
    logits = jnp.dot(normed_rows, router_w, preferred_element_type=jnp.float32)
    match = chosen[:, :, None] == jnp.arange(logits.shape[1], dtype=jnp.int32)[None, None, :]
    picked = jnp.sum(jnp.where(match, logits[:, None, :], jnp.zeros((), logits.dtype)), axis=-1)
    squashed = jax.nn.sigmoid(picked)
    return squashed / jnp.sum(squashed, axis=-1, keepdims=True)


def slot_ranks(chosen, block_rows, experts):
    blocks = chosen.shape[0] // block_rows
    width = block_rows * chosen.shape[1]
    grouped = chosen.reshape(blocks, width)
    hits = (grouped[:, :, None] == jnp.arange(experts, dtype=jnp.int32)[None, None, :]).astype(
        jnp.bfloat16
    )
    lower = jnp.arange(width)[:, None] >= jnp.arange(width)[None, :]
    counts = jnp.einsum(
        "ij,bje->bie", lower.astype(jnp.bfloat16), hits, preferred_element_type=jnp.float32
    )
    ranks = jnp.sum(counts * hits.astype(jnp.float32), axis=-1) - 1
    return ranks.astype(jnp.int32).reshape(chosen.shape)


def expert_group(rows, gate_up, down):
    both = jnp.einsum("gsd,dxf->gsxf", rows, gate_up, preferred_element_type=jnp.float32)
    hidden = (jax.nn.silu(both[..., 0, :]) * both[..., 1, :]).astype(jnp.bfloat16)
    return jnp.einsum("gsf,fd->gsd", hidden, down, preferred_element_type=jnp.float32).astype(
        jnp.bfloat16
    )


def scatter_rows(normed_rows, slot_index, buffer_rows):
    slots = jnp.arange(buffer_rows, dtype=jnp.int32)
    select = jnp.sum(
        (slot_index[None, :, :] == slots[:, None, None]).astype(jnp.bfloat16), axis=-1
    )
    return jnp.dot(select, normed_rows, preferred_element_type=jnp.float32).astype(jnp.bfloat16)


def combine_rows(out_table, slot_index, gate_vals):
    slots = jnp.arange(out_table.shape[0], dtype=jnp.int32)
    weights = jnp.sum(
        jnp.where(slot_index[:, :, None] == slots[None, None, :], gate_vals[:, :, None], 0.0),
        axis=1,
    )
    high = weights.astype(jnp.bfloat16)
    low = (weights - high.astype(jnp.float32)).astype(jnp.bfloat16)
    return jnp.dot(high, out_table, preferred_element_type=jnp.float32) + jnp.dot(
        low, out_table, preferred_element_type=jnp.float32
    )


def seq_shift(x, shift, size):
    return lax.ppermute(x, "seq", [(i, (i + shift) % size) for i in range(size)])


def paired_shift(x, local, seq_size, exp_size, back):
    pairs = []
    for s in range(seq_size):
        for e in range(exp_size):
            step = 1 if e % 2 == 0 else -1
            if back:
                step = -step
            pairs.append((s * exp_size + e, ((s + step) % seq_size) * exp_size + e))
    return lax.ppermute(x, ("seq", "exp"), pairs)


def on_device(resid, qkv, w_out, norm_gain, router_w, expert_ids, w_gate_up, w_down):
    row_count = resid.shape[1]
    model_width = resid.shape[2]
    seq_size = lax.axis_size("seq")
    exp_size = lax.axis_size("exp")
    me = lax.axis_index("seq")
    seq_length = row_count * seq_size
    head_local = H // seq_size
    local_width = head_local * HD
    packed = qkv[0].reshape(row_count, 3, seq_size, local_width)
    pieces = []
    for shift in range(seq_size):
        target = (me + shift) % seq_size
        piece = lax.dynamic_index_in_dim(packed, target, axis=2, keepdims=False)
        pieces.append(piece if shift == 0 else seq_shift(piece, shift, seq_size))
    regrouped = jnp.stack(pieces, axis=0).reshape(seq_length, 3, local_width)
    queries = regrouped[:, 0].reshape(seq_length, head_local, HD)
    keys_all = regrouped[:, 1].reshape(seq_length, head_local, HD)
    values_all = regrouped[:, 2].reshape(seq_length, head_local, HD)
    scores = jnp.einsum(
        "qhd,khd->hqk", queries, keys_all, preferred_element_type=jnp.float32
    ) / math.sqrt(HD)
    weights = jax.nn.softmax(scores, axis=-1).astype(jnp.bfloat16)
    attended = jnp.einsum(
        "hqk,khd->qhd", weights, values_all, preferred_element_type=jnp.float32
    ).reshape(seq_length, local_width).astype(jnp.bfloat16)
    partial = jnp.dot(attended, w_out, preferred_element_type=jnp.float32).reshape(
        seq_size, row_count, model_width
    )
    projected = partial[0]
    for shift in range(1, seq_size):
        projected = projected + seq_shift(
            partial[shift].astype(jnp.bfloat16), -shift, seq_size
        ).astype(jnp.float32)
    mixed = resid[0].astype(jnp.float32) + projected
    meansq = jnp.mean(mixed * mixed, axis=-1, keepdims=True)
    normed = (mixed * lax.rsqrt(meansq + epsilon) * norm_gain).astype(jnp.bfloat16)
    exp_local = w_gate_up.shape[0]
    slot_cap = row_count // 8
    gathered = jnp.concatenate(
        [normed] + [seq_shift(normed, shift, seq_size) for shift in range(1, seq_size)], axis=0
    ).reshape(seq_size, row_count, model_width)
    far = seq_size // 2
    blocks_abs = (me - jnp.arange(seq_size, dtype=jnp.int32)) % seq_size
    chosen_all = jnp.take(expert_ids[0].reshape(seq_size, row_count, -1), blocks_abs, axis=0)
    direct_rows = jnp.concatenate([gathered[0], gathered[far]], axis=0)
    chosen = jnp.concatenate([chosen_all[0], chosen_all[far]], axis=0)
    gate_vals = gate_weights(direct_rows, router_w, chosen)
    ranks = slot_ranks(chosen, row_count, EXPERTS)
    kind = (jnp.arange(2 * row_count, dtype=jnp.int32) // row_count)[:, None]
    owner = chosen // exp_local
    local_of = chosen % exp_local
    slot_index = ((local_of * exp_size + owner) * 2 + kind) * slot_cap + ranks
    grid = (exp_local, exp_size, 2 * slot_cap)
    slot_ids = jnp.arange(math.prod(grid), dtype=jnp.int32).reshape(grid)
    select = jnp.sum(
        (slot_index[None, None, None, :, :] == slot_ids[..., None, None]).astype(
            jnp.bfloat16
        ),
        axis=-1,
    )
    outgoing = jnp.einsum(
        "cgsp,pd->cgsd", select, direct_rows, preferred_element_type=jnp.float32
    ).astype(jnp.bfloat16)
    homes = []
    for local in range(exp_local):
        received = lax.all_to_all(outgoing[local], "exp", split_axis=0, concat_axis=0, tiled=True)
        forwarded = paired_shift(received, local, seq_size, exp_size, False)
        mine = expert_group(received, w_gate_up[local], w_down[local])
        theirs = expert_group(forwarded, w_gate_up[local], w_down[local])
        returned = paired_shift(theirs, local, seq_size, exp_size, True)
        pair_sum = (mine.astype(jnp.float32) + returned.astype(jnp.float32)).astype(jnp.bfloat16)
        homes.append(lax.all_to_all(pair_sum, "exp", split_axis=0, concat_axis=0, tiled=True))
    weights = jnp.sum(
        jnp.where(
            slot_index[:, :, None, None, None] == slot_ids[None, None],
            gate_vals[:, :, None, None, None],
            0.0,
        ),
        axis=1,
    )
    high = weights.astype(jnp.bfloat16)
    low = (weights - high.astype(jnp.float32)).astype(jnp.bfloat16)
    expert_sum = None
    for local in range(exp_local):
        part = jnp.einsum(
            "pgs,gsd->pd", high[:, local], homes[local], preferred_element_type=jnp.float32
        ) + jnp.einsum(
            "pgs,gsd->pd", low[:, local], homes[local], preferred_element_type=jnp.float32
        )
        far_part = seq_shift(part[row_count:].astype(jnp.bfloat16), far, seq_size)
        part = part[:row_count] + far_part.astype(jnp.float32)
        expert_sum = part if expert_sum is None else expert_sum + part
    return (mixed + expert_sum).astype(jnp.bfloat16).reshape(1, row_count, model_width)


def solution(mesh):
    in_specs = (
        P("exp", "seq", None),
        P("exp", "seq", None),
        P("seq", None),
        P(),
        P(),
        P("exp", None, None),
        P("exp", None, None, "seq"),
        P("exp", "seq", None),
    )
    out_specs = P("exp", "seq", None)
    return jax.shard_map(
        on_device, mesh=mesh, in_specs=in_specs, out_specs=out_specs, check_vma=False
    )
```

```python
import math

import jax
import jax.numpy as jnp
from jax import lax
from jax.sharding import PartitionSpec as P

H = 16
HD = 128
EXPERTS = 64


epsilon = 1e-05


def gate_weights(normed_rows, router_w, chosen):
    logits = jnp.dot(normed_rows, router_w, preferred_element_type=jnp.float32)
    match = chosen[:, :, None] == jnp.arange(logits.shape[1], dtype=jnp.int32)[None, None, :]
    picked = jnp.sum(jnp.where(match, logits[:, None, :], jnp.zeros((), logits.dtype)), axis=-1)
    squashed = jax.nn.sigmoid(picked)
    return squashed / jnp.sum(squashed, axis=-1, keepdims=True)


def slot_ranks(chosen, block_rows, experts):
    blocks = chosen.shape[0] // block_rows
    width = block_rows * chosen.shape[1]
    grouped = chosen.reshape(blocks, width)
    hits = (grouped[:, :, None] == jnp.arange(experts, dtype=jnp.int32)[None, None, :]).astype(
        jnp.bfloat16
    )
    lower = jnp.arange(width)[:, None] >= jnp.arange(width)[None, :]
    counts = jnp.einsum(
        "ij,bje->bie", lower.astype(jnp.bfloat16), hits, preferred_element_type=jnp.float32
    )
    ranks = jnp.sum(counts * hits.astype(jnp.float32), axis=-1) - 1
    return ranks.astype(jnp.int32).reshape(chosen.shape)


def expert_group(rows, gate_up, down):
    both = jnp.einsum("gsd,dxf->gsxf", rows, gate_up, preferred_element_type=jnp.float32)
    hidden = (jax.nn.silu(both[..., 0, :]) * both[..., 1, :]).astype(jnp.bfloat16)
    return jnp.einsum("gsf,fd->gsd", hidden, down, preferred_element_type=jnp.float32).astype(
        jnp.bfloat16
    )


def scatter_rows(normed_rows, slot_index, buffer_rows):
    slots = jnp.arange(buffer_rows, dtype=jnp.int32)
    select = jnp.sum(
        (slot_index[None, :, :] == slots[:, None, None]).astype(jnp.bfloat16), axis=-1
    )
    return jnp.dot(select, normed_rows, preferred_element_type=jnp.float32).astype(jnp.bfloat16)


def combine_rows(out_table, slot_index, gate_vals):
    slots = jnp.arange(out_table.shape[0], dtype=jnp.int32)
    weights = jnp.sum(
        jnp.where(slot_index[:, :, None] == slots[None, None, :], gate_vals[:, :, None], 0.0),
        axis=1,
    )
    high = weights.astype(jnp.bfloat16)
    low = (weights - high.astype(jnp.float32)).astype(jnp.bfloat16)
    return jnp.dot(high, out_table, preferred_element_type=jnp.float32) + jnp.dot(
        low, out_table, preferred_element_type=jnp.float32
    )


def seq_shift(x, shift, size):
    return lax.ppermute(x, "seq", [(i, (i + shift) % size) for i in range(size)])


def paired_shift(x, local, seq_size, exp_size, back):
    pairs = []
    for s in range(seq_size):
        for e in range(exp_size):
            step = 1 if e % 2 == 0 else -1
            if back:
                step = -step
            pairs.append((s * exp_size + e, ((s + step) % seq_size) * exp_size + e))
    return lax.ppermute(x, ("seq", "exp"), pairs)


def on_device(resid, qkv, w_out, norm_gain, router_w, expert_ids, w_gate_up, w_down):
    row_count = resid.shape[1]
    model_width = resid.shape[2]
    seq_size = lax.axis_size("seq")
    exp_size = lax.axis_size("exp")
    me = lax.axis_index("seq")
    seq_length = row_count * seq_size
    head_local = H // seq_size
    local_width = head_local * HD
    packed = qkv[0].reshape(row_count, 3, seq_size, local_width)
    pieces = []
    for shift in range(seq_size):
        target = (me + shift) % seq_size
        piece = lax.dynamic_index_in_dim(packed, target, axis=2, keepdims=False)
        pieces.append(piece if shift == 0 else seq_shift(piece, shift, seq_size))
    regrouped = jnp.stack(pieces, axis=0).reshape(seq_length, 3, local_width)
    queries = regrouped[:, 0].reshape(seq_length, head_local, HD)
    keys_all = regrouped[:, 1].reshape(seq_length, head_local, HD)
    values_all = regrouped[:, 2].reshape(seq_length, head_local, HD)
    scores = jnp.einsum(
        "qhd,khd->hqk", queries, keys_all, preferred_element_type=jnp.float32
    ) / math.sqrt(HD)
    weights = jax.nn.softmax(scores, axis=-1).astype(jnp.bfloat16)
    attended = jnp.einsum(
        "hqk,khd->qhd", weights, values_all, preferred_element_type=jnp.float32
    ).reshape(seq_length, local_width).astype(jnp.bfloat16)
    partial = jnp.dot(attended, w_out, preferred_element_type=jnp.float32).reshape(
        seq_size, row_count, model_width
    )
    projected = partial[0]
    for shift in range(1, seq_size):
        projected = projected + seq_shift(
            partial[shift].astype(jnp.bfloat16), -shift, seq_size
        ).astype(jnp.float32)
    mixed = resid[0].astype(jnp.float32) + projected
    meansq = jnp.mean(mixed * mixed, axis=-1, keepdims=True)
    normed = (mixed * lax.rsqrt(meansq + epsilon) * norm_gain).astype(jnp.bfloat16)
    exp_local = w_gate_up.shape[0]
    slot_cap = row_count // 8
    gathered = jnp.concatenate(
        [normed] + [seq_shift(normed, shift, seq_size) for shift in range(1, seq_size)], axis=0
    )
    far = seq_size // 2
    blocks_abs = (me - jnp.arange(seq_size, dtype=jnp.int32)) % seq_size
    chosen = jnp.take(expert_ids[0].reshape(seq_size, row_count, -1), blocks_abs, axis=0).reshape(
        seq_length, -1
    )
    gate_vals = gate_weights(gathered, router_w, chosen)
    ranks = slot_ranks(chosen, row_count, EXPERTS)
    owner = chosen // exp_local
    local_of = chosen % exp_local
    block_of = (jnp.arange(seq_length, dtype=jnp.int32) // row_count)[:, None]
    kind = block_of // far
    direct = row_count * far
    block_rows = gathered.reshape(seq_size, row_count, model_width)
    direct_rows = jnp.concatenate([block_rows[0], block_rows[far]], axis=0)
    direct_index = jnp.concatenate([chosen[:row_count], chosen[direct : direct + row_count]], 0)
    direct_ranks = jnp.concatenate([ranks[:row_count], ranks[direct : direct + row_count]], 0)
    direct_kind = (jnp.arange(2 * row_count, dtype=jnp.int32) // row_count)[:, None]
    direct_slot = (
        ((direct_index % exp_local) * exp_size + direct_index // exp_local) * 2 + direct_kind
    ) * slot_cap + direct_ranks
    grid = (exp_local, exp_size, 2 * slot_cap)
    slot_ids = jnp.arange(math.prod(grid), dtype=jnp.int32).reshape(grid)
    select = jnp.sum(
        (direct_slot[None, None, None, :, :] == slot_ids[..., None, None]).astype(jnp.bfloat16),
        axis=-1,
    )
    outgoing = jnp.einsum(
        "cgsp,pd->cgsd", select, direct_rows, preferred_element_type=jnp.float32
    ).astype(jnp.bfloat16)
    received = lax.all_to_all(outgoing[0], "exp", split_axis=0, concat_axis=0, tiled=True)
    forwarded = paired_shift(received, 0, seq_size, exp_size, False)
    mine = expert_group(received, w_gate_up[0], w_down[0])
    theirs = expert_group(forwarded, w_gate_up[0], w_down[0])
    home_first = lax.all_to_all(
        jnp.stack([mine, theirs], axis=0), "exp", split_axis=1, concat_axis=1, tiled=True
    )
    received = lax.all_to_all(outgoing[1], "exp", split_axis=0, concat_axis=0, tiled=True)
    forwarded = paired_shift(received, 1, seq_size, exp_size, False)
    mine = expert_group(received, w_gate_up[1], w_down[1])
    theirs = expert_group(forwarded, w_gate_up[1], w_down[1])
    returned = paired_shift(theirs, 1, seq_size, exp_size, True)
    pair_sum = (mine.astype(jnp.float32) + returned.astype(jnp.float32)).astype(jnp.bfloat16)
    home_second = lax.all_to_all(pair_sum, "exp", split_axis=0, concat_axis=0, tiled=True)
    step = jnp.where(owner % 2 == 0, 1, seq_size - 1)
    neighbour_kind = jnp.where(block_of == step, 0, 1)
    is_direct = block_of % far == 0
    first_slot = (
        (jnp.where(is_direct, 0, 1) * exp_size + owner) * 2
        + jnp.where(is_direct, kind, neighbour_kind)
    ) * slot_cap + ranks
    first_ids = jnp.arange(2 * exp_size * 2 * slot_cap, dtype=jnp.int32).reshape(
        2, exp_size, 2 * slot_cap
    )
    first_weights = jnp.sum(
        jnp.where(
            (first_slot[:, :, None, None, None] == first_ids[None, None]) & (local_of == 0)[
                :, :, None, None, None
            ],
            gate_vals[:, :, None, None, None],
            0.0,
        ),
        axis=1,
    )
    second_slot = (owner * 2 + kind) * slot_cap + ranks
    second_ids = jnp.arange(exp_size * 2 * slot_cap, dtype=jnp.int32).reshape(
        exp_size, 2 * slot_cap
    )
    second_gates = jnp.concatenate(
        [gate_vals[:row_count], gate_vals[direct : direct + row_count]], 0
    )
    second_weights = jnp.sum(
        jnp.where(
            (
                (jnp.concatenate([second_slot[:row_count], second_slot[direct : direct + row_count]], 0)[:, :, None, None] == second_ids[None, None])
                & (direct_index % exp_local == 1)[:, :, None, None]
            ),
            second_gates[:, :, None, None],
            0.0,
        ),
        axis=1,
    )

    def weighted(weights, table, spec):
        high = weights.astype(jnp.bfloat16)
        low = (weights - high.astype(jnp.float32)).astype(jnp.bfloat16)
        return jnp.einsum(spec, high, table, preferred_element_type=jnp.float32) + jnp.einsum(
            spec, low, table, preferred_element_type=jnp.float32
        )

    first = weighted(first_weights, home_first, "pags,agsd->pd").reshape(
        seq_size, row_count, model_width
    )
    second = weighted(second_weights, home_second, "pgs,gsd->pd")
    expert_sum = first[0] + second[:row_count]
    for shift in range(1, seq_size):
        piece = first[shift]
        if shift == far:
            piece = piece + second[row_count:]
        expert_sum = expert_sum + seq_shift(
            piece.astype(jnp.bfloat16), -shift, seq_size
        ).astype(jnp.float32)
    return (mixed + expert_sum).astype(jnp.bfloat16).reshape(1, row_count, model_width)


def solution(mesh):
    in_specs = (
        P("exp", "seq", None),
        P("exp", "seq", None),
        P("seq", None),
        P(),
        P(),
        P("exp", None, None),
        P("exp", None, None, "seq"),
        P("exp", "seq", None),
    )
    out_specs = P("exp", "seq", None)
    return jax.shard_map(
        on_device, mesh=mesh, in_specs=in_specs, out_specs=out_specs, check_vma=False
    )
```

```python
import math

import jax
import jax.numpy as jnp
from jax import lax
from jax.sharding import PartitionSpec as P


H = 16
HD = 128
EXPERTS = 64


epsilon = 1e-05


def gate_weights(normed_rows, router_w, chosen):
    logits = jnp.dot(normed_rows, router_w, preferred_element_type=jnp.float32)
    match = chosen[:, :, None] == jnp.arange(logits.shape[1], dtype=jnp.int32)[None, None, :]
    picked = jnp.sum(jnp.where(match, logits[:, None, :], jnp.zeros((), logits.dtype)), axis=-1)
    squashed = jax.nn.sigmoid(picked)
    return squashed / jnp.sum(squashed, axis=-1, keepdims=True)


def slot_ranks(chosen, block_rows, experts):
    blocks = chosen.shape[0] // block_rows
    width = block_rows * chosen.shape[1]
    grouped = chosen.reshape(blocks, width)
    hits = (grouped[:, :, None] == jnp.arange(experts, dtype=jnp.int32)[None, None, :]).astype(
        jnp.bfloat16
    )
    lower = jnp.arange(width)[:, None] >= jnp.arange(width)[None, :]
    counts = jnp.einsum(
        "ij,bje->bie", lower.astype(jnp.bfloat16), hits, preferred_element_type=jnp.float32
    )
    ranks = jnp.sum(counts * hits.astype(jnp.float32), axis=-1) - 1
    return ranks.astype(jnp.int32).reshape(chosen.shape)


def expert_group(rows, gate_up, down):
    both = jnp.einsum("gsd,dxf->gsxf", rows, gate_up, preferred_element_type=jnp.float32)
    hidden = (jax.nn.silu(both[..., 0, :]) * both[..., 1, :]).astype(jnp.bfloat16)
    return jnp.einsum("gsf,fd->gsd", hidden, down, preferred_element_type=jnp.float32).astype(
        jnp.bfloat16
    )


def seq_shift(x, shift, size):
    return lax.ppermute(x, "seq", [(i, (i + shift) % size) for i in range(size)])


def paired_shift(x, seq_size, exp_size, back):
    pairs = []
    for s in range(seq_size):
        for e in range(exp_size):
            step = 1 if e % 2 == 0 else -1
            if back:
                step = -step
            pairs.append((s * exp_size + e, ((s + step) % seq_size) * exp_size + e))
    return lax.ppermute(x, ("seq", "exp"), pairs)


def on_device(resid, qkv, w_out, norm_gain, router_w, expert_ids, w_gate_up, w_down):
    row_count = resid.shape[1]
    model_width = resid.shape[2]
    seq_size = lax.axis_size("seq")
    exp_size = lax.axis_size("exp")
    me = lax.axis_index("seq")
    seq_length = row_count * seq_size
    head_local = H // seq_size
    local_width = head_local * HD
    packed = qkv[0].reshape(row_count, 3, seq_size, local_width)
    pieces = []
    for shift in range(seq_size):
        target = (me + shift) % seq_size
        piece = lax.dynamic_index_in_dim(packed, target, axis=2, keepdims=False)
        pieces.append(piece if shift == 0 else seq_shift(piece, shift, seq_size))
    regrouped = jnp.stack(pieces, axis=0).reshape(seq_length, 3, local_width)
    queries = regrouped[:, 0].reshape(seq_length, head_local, HD)
    keys_all = regrouped[:, 1].reshape(seq_length, head_local, HD)
    values_all = regrouped[:, 2].reshape(seq_length, head_local, HD)
    scores = jnp.einsum(
        "qhd,khd->hqk", queries, keys_all, preferred_element_type=jnp.float32
    ) / math.sqrt(HD)
    weights = jax.nn.softmax(scores, axis=-1).astype(jnp.bfloat16)
    attended = jnp.einsum(
        "hqk,khd->qhd", weights, values_all, preferred_element_type=jnp.float32
    ).reshape(seq_length, local_width).astype(jnp.bfloat16)
    partial = jnp.dot(attended, w_out, preferred_element_type=jnp.float32).reshape(
        seq_size, row_count, model_width
    )
    projected = partial[0]
    for shift in range(1, seq_size):
        projected = projected + seq_shift(
            partial[shift].astype(jnp.bfloat16), -shift, seq_size
        ).astype(jnp.float32)
    mixed = resid[0].astype(jnp.float32) + projected
    meansq = jnp.mean(mixed * mixed, axis=-1, keepdims=True)
    normed = (mixed * lax.rsqrt(meansq + epsilon) * norm_gain).astype(jnp.bfloat16)
    exp_local = w_gate_up.shape[0]
    slot_cap = row_count // 8
    gathered = jnp.concatenate(
        [normed] + [seq_shift(normed, shift, seq_size) for shift in range(1, seq_size)], axis=0
    )
    far = seq_size // 2
    blocks_abs = (me - jnp.arange(seq_size, dtype=jnp.int32)) % seq_size
    chosen = jnp.take(expert_ids[0].reshape(seq_size, row_count, -1), blocks_abs, axis=0).reshape(
        seq_length, -1
    )
    gate_vals = gate_weights(gathered, router_w, chosen)
    ranks = slot_ranks(chosen, row_count, EXPERTS)
    owner = chosen // exp_local
    local_of = chosen % exp_local
    block_of = (jnp.arange(seq_length, dtype=jnp.int32) // row_count)[:, None]
    kind = block_of // far
    direct = row_count * far
    block_rows = gathered.reshape(seq_size, row_count, model_width)
    direct_rows = jnp.concatenate([block_rows[0], block_rows[far]], axis=0)
    direct_index = jnp.concatenate([chosen[:row_count], chosen[direct : direct + row_count]], 0)
    direct_ranks = jnp.concatenate([ranks[:row_count], ranks[direct : direct + row_count]], 0)
    direct_kind = (jnp.arange(2 * row_count, dtype=jnp.int32) // row_count)[:, None]
    direct_slot = (
        ((direct_index % exp_local) * exp_size + direct_index // exp_local) * 2 + direct_kind
    ) * slot_cap + direct_ranks
    grid = (exp_local, exp_size, 2 * slot_cap)
    slot_ids = jnp.arange(math.prod(grid), dtype=jnp.int32).reshape(grid)
    select = jnp.sum(
        (direct_slot[None, None, None, :, :] == slot_ids[..., None, None]).astype(jnp.bfloat16),
        axis=-1,
    )
    outgoing = jnp.einsum(
        "cgsp,pd->cgsd", select, direct_rows, preferred_element_type=jnp.float32
    ).astype(jnp.bfloat16)
    received = lax.all_to_all(outgoing[0], "exp", split_axis=0, concat_axis=0, tiled=True)
    forwarded = paired_shift(received, seq_size, exp_size, False)
    mine = expert_group(received, w_gate_up[0], w_down[0])
    theirs = expert_group(forwarded, w_gate_up[0], w_down[0])
    home_first = lax.all_to_all(
        jnp.stack([mine, theirs], axis=0), "exp", split_axis=1, concat_axis=1, tiled=True
    )
    received = lax.all_to_all(outgoing[1], "exp", split_axis=0, concat_axis=0, tiled=True)
    forwarded = paired_shift(received, seq_size, exp_size, False)
    mine = expert_group(received, w_gate_up[1], w_down[1])
    theirs = expert_group(forwarded, w_gate_up[1], w_down[1])
    returned = paired_shift(theirs, seq_size, exp_size, True)
    pair_sum = (mine.astype(jnp.float32) + returned.astype(jnp.float32)).astype(jnp.bfloat16)
    home_second = lax.all_to_all(pair_sum, "exp", split_axis=0, concat_axis=0, tiled=True)
    step = jnp.where(owner % 2 == 0, 1, seq_size - 1)
    neighbour_kind = jnp.where(block_of == step, 0, 1)
    is_direct = block_of % far == 0
    first_slot = (
        (jnp.where(is_direct, 0, 1) * exp_size + owner) * 2
        + jnp.where(is_direct, kind, neighbour_kind)
    ) * slot_cap + ranks
    first_ids = jnp.arange(2 * exp_size * 2 * slot_cap, dtype=jnp.int32).reshape(
        2, exp_size, 2 * slot_cap
    )
    first_weights = jnp.sum(
        jnp.where(
            (first_slot[:, :, None, None, None] == first_ids[None, None]) & (local_of == 0)[
                :, :, None, None, None
            ],
            gate_vals[:, :, None, None, None],
            0.0,
        ),
        axis=1,
    )
    second_slot = (owner * 2 + kind) * slot_cap + ranks
    second_ids = jnp.arange(exp_size * 2 * slot_cap, dtype=jnp.int32).reshape(
        exp_size, 2 * slot_cap
    )
    second_gates = jnp.concatenate(
        [gate_vals[:row_count], gate_vals[direct : direct + row_count]], 0
    )
    second_weights = jnp.sum(
        jnp.where(
            (
                (jnp.concatenate([second_slot[:row_count], second_slot[direct : direct + row_count]], 0)[:, :, None, None] == second_ids[None, None])
                & (direct_index % exp_local == 1)[:, :, None, None]
            ),
            second_gates[:, :, None, None],
            0.0,
        ),
        axis=1,
    )

    def weighted(weights, table, spec):
        high = weights.astype(jnp.bfloat16)
        low = (weights - high.astype(jnp.float32)).astype(jnp.bfloat16)
        return jnp.einsum(spec, high, table, preferred_element_type=jnp.float32) + jnp.einsum(
            spec, low, table, preferred_element_type=jnp.float32
        )

    first = weighted(first_weights, home_first, "pags,agsd->pd").reshape(
        seq_size, row_count, model_width
    )
    second = weighted(second_weights, home_second, "pgs,gsd->pd")
    expert_sum = first[0] + second[:row_count]
    for shift in range(1, seq_size):
        piece = first[shift]
        if shift == far:
            piece = piece + second[row_count:]
        expert_sum = expert_sum + seq_shift(
            piece.astype(jnp.bfloat16), -shift, seq_size
        ).astype(jnp.float32)
    return (mixed + expert_sum).astype(jnp.bfloat16).reshape(1, row_count, model_width)


def solution(mesh):
    in_specs = (
        P("exp", "seq", None),
        P("exp", "seq", None),
        P("seq", None),
        P(),
        P(),
        P("exp", None, None),
        P("exp", None, None, "seq"),
        P("exp", "seq", None),
    )
    out_specs = P("exp", "seq", None)

    return jax.shard_map(on_device, mesh=mesh, in_specs=in_specs, out_specs=out_specs, check_vma=False)
```

```python
import math

import jax
import jax.numpy as jnp
from jax import lax
from jax.sharding import PartitionSpec as P


H = 16
HD = 128
EXPERTS = 64


epsilon = 1e-05


def gate_weights(normed_rows, router_w, chosen):
    logits = jnp.dot(normed_rows, router_w, preferred_element_type=jnp.float32)
    match = chosen[:, :, None] == jnp.arange(logits.shape[1], dtype=jnp.int32)[None, None, :]
    picked = jnp.sum(jnp.where(match, logits[:, None, :], jnp.zeros((), logits.dtype)), axis=-1)
    squashed = jax.nn.sigmoid(picked)
    return squashed / jnp.sum(squashed, axis=-1, keepdims=True)


def slot_ranks(chosen, block_rows, experts):
    blocks = chosen.shape[0] // block_rows
    width = block_rows * chosen.shape[1]
    grouped = chosen.reshape(blocks, width)
    hits = (grouped[:, :, None] == jnp.arange(experts, dtype=jnp.int32)[None, None, :]).astype(
        jnp.bfloat16
    )
    lower = jnp.arange(width)[:, None] >= jnp.arange(width)[None, :]
    counts = jnp.einsum(
        "ij,bje->bie", lower.astype(jnp.bfloat16), hits, preferred_element_type=jnp.float32
    )
    ranks = jnp.sum(counts * hits.astype(jnp.float32), axis=-1) - 1
    return ranks.astype(jnp.int32).reshape(chosen.shape)


def expert_group(rows, gate_up, down):
    both = jnp.einsum("gsd,dxf->gsxf", rows, gate_up, preferred_element_type=jnp.float32)
    hidden = (jax.nn.silu(both[..., 0, :]) * both[..., 1, :]).astype(jnp.bfloat16)
    return jnp.einsum("gsf,fd->gsd", hidden, down, preferred_element_type=jnp.float32).astype(
        jnp.bfloat16
    )


def gate_tables(first_slot, local_of, gate_vals, first_ids, second_slot, second_ids, direct_index, row_count, direct, exp_local):
    first_weights = jnp.sum(
        jnp.where(
            (first_slot[:, :, None, None, None] == first_ids[None, None]) & (local_of == 0)[
                :, :, None, None, None
            ],
            gate_vals[:, :, None, None, None],
            0.0,
        ),
        axis=1,
    )
    second_gates = jnp.concatenate(
        [gate_vals[:row_count], gate_vals[direct : direct + row_count]], 0
    )
    second_weights = jnp.sum(
        jnp.where(
            (
                (jnp.concatenate([second_slot[:row_count], second_slot[direct : direct + row_count]], 0)[:, :, None, None] == second_ids[None, None])
                & (direct_index % exp_local == 1)[:, :, None, None]
            ),
            second_gates[:, :, None, None],
            0.0,
        ),
        axis=1,
    )

    return first_weights, second_weights


def seq_shift(x, shift, size):
    return lax.ppermute(x, "seq", [(i, (i + shift) % size) for i in range(size)])


def paired_shift(x, seq_size, exp_size, back):
    pairs = []
    for s in range(seq_size):
        for e in range(exp_size):
            step = 1 if e % 2 == 0 else -1
            if back:
                step = -step
            pairs.append((s * exp_size + e, ((s + step) % seq_size) * exp_size + e))
    return lax.ppermute(x, ("seq", "exp"), pairs)


def on_device(resid, qkv, w_out, norm_gain, router_w, expert_ids, w_gate_up, w_down):
    row_count = resid.shape[1]
    model_width = resid.shape[2]
    seq_size = lax.axis_size("seq")
    exp_size = lax.axis_size("exp")
    me = lax.axis_index("seq")
    seq_length = row_count * seq_size
    head_local = H // seq_size
    local_width = head_local * HD
    packed = qkv[0].reshape(row_count, 3, seq_size, local_width)
    pieces = []
    for shift in range(seq_size):
        target = (me + shift) % seq_size
        piece = lax.dynamic_index_in_dim(packed, target, axis=2, keepdims=False)
        pieces.append(piece if shift == 0 else seq_shift(piece, shift, seq_size))
    regrouped = jnp.stack(pieces, axis=0).reshape(seq_length, 3, local_width)
    queries = regrouped[:, 0].reshape(seq_length, head_local, HD)
    keys_all = regrouped[:, 1].reshape(seq_length, head_local, HD)
    values_all = regrouped[:, 2].reshape(seq_length, head_local, HD)
    scores = jnp.einsum(
        "qhd,khd->hqk", queries, keys_all, preferred_element_type=jnp.float32
    ) / math.sqrt(HD)
    weights = jax.nn.softmax(scores, axis=-1).astype(jnp.bfloat16)
    attended = jnp.einsum(
        "hqk,khd->qhd", weights, values_all, preferred_element_type=jnp.float32
    ).reshape(seq_length, local_width).astype(jnp.bfloat16)
    partial = jnp.dot(attended, w_out, preferred_element_type=jnp.float32).reshape(
        seq_size, row_count, model_width
    )
    projected = partial[0]
    for shift in range(1, seq_size):
        projected = projected + seq_shift(
            partial[shift].astype(jnp.bfloat16), -shift, seq_size
        ).astype(jnp.float32)
    mixed = resid[0].astype(jnp.float32) + projected
    meansq = jnp.mean(mixed * mixed, axis=-1, keepdims=True)
    normed = (mixed * lax.rsqrt(meansq + epsilon) * norm_gain).astype(jnp.bfloat16)
    exp_local = w_gate_up.shape[0]
    slot_cap = row_count // 8
    gathered = jnp.concatenate(
        [normed] + [seq_shift(normed, shift, seq_size) for shift in range(1, seq_size)], axis=0
    )
    far = seq_size // 2
    blocks_abs = (me - jnp.arange(seq_size, dtype=jnp.int32)) % seq_size
    chosen = jnp.take(expert_ids[0].reshape(seq_size, row_count, -1), blocks_abs, axis=0).reshape(
        seq_length, -1
    )
    gate_vals = gate_weights(gathered, router_w, chosen)
    ranks = slot_ranks(chosen, row_count, EXPERTS)
    owner = chosen // exp_local
    local_of = chosen % exp_local
    block_of = (jnp.arange(seq_length, dtype=jnp.int32) // row_count)[:, None]
    kind = block_of // far
    direct = row_count * far
    block_rows = gathered.reshape(seq_size, row_count, model_width)
    direct_rows = jnp.concatenate([block_rows[0], block_rows[far]], axis=0)
    direct_index = jnp.concatenate([chosen[:row_count], chosen[direct : direct + row_count]], 0)
    direct_ranks = jnp.concatenate([ranks[:row_count], ranks[direct : direct + row_count]], 0)
    direct_kind = (jnp.arange(2 * row_count, dtype=jnp.int32) // row_count)[:, None]
    direct_slot = (
        ((direct_index % exp_local) * exp_size + direct_index // exp_local) * 2 + direct_kind
    ) * slot_cap + direct_ranks
    grid = (exp_local, exp_size, 2 * slot_cap)
    slot_ids = jnp.arange(math.prod(grid), dtype=jnp.int32).reshape(grid)
    select = jnp.sum(
        (direct_slot[None, None, None, :, :] == slot_ids[..., None, None]).astype(jnp.bfloat16),
        axis=-1,
    )
    outgoing = jnp.einsum(
        "cgsp,pd->cgsd", select, direct_rows, preferred_element_type=jnp.float32
    ).astype(jnp.bfloat16)
    received = lax.all_to_all(outgoing[0], "exp", split_axis=0, concat_axis=0, tiled=True)
    forwarded = paired_shift(received, seq_size, exp_size, False)
    mine = expert_group(received, w_gate_up[0], w_down[0])
    theirs = expert_group(forwarded, w_gate_up[0], w_down[0])
    home_first = lax.all_to_all(
        jnp.stack([mine, theirs], axis=0), "exp", split_axis=1, concat_axis=1, tiled=True
    )
    received = lax.all_to_all(outgoing[1], "exp", split_axis=0, concat_axis=0, tiled=True)
    forwarded = paired_shift(received, seq_size, exp_size, False)
    mine = expert_group(received, w_gate_up[1], w_down[1])
    theirs = expert_group(forwarded, w_gate_up[1], w_down[1])
    returned = paired_shift(theirs, seq_size, exp_size, True)
    pair_sum = (mine.astype(jnp.float32) + returned.astype(jnp.float32)).astype(jnp.bfloat16)
    home_second = lax.all_to_all(pair_sum, "exp", split_axis=0, concat_axis=0, tiled=True)
    step = jnp.where(owner % 2 == 0, 1, seq_size - 1)
    neighbour_kind = jnp.where(block_of == step, 0, 1)
    is_direct = block_of % far == 0
    first_slot = (
        (jnp.where(is_direct, 0, 1) * exp_size + owner) * 2
        + jnp.where(is_direct, kind, neighbour_kind)
    ) * slot_cap + ranks
    first_ids = jnp.arange(2 * exp_size * 2 * slot_cap, dtype=jnp.int32).reshape(
        2, exp_size, 2 * slot_cap
    )
    second_slot = (owner * 2 + kind) * slot_cap + ranks
    second_ids = jnp.arange(exp_size * 2 * slot_cap, dtype=jnp.int32).reshape(
        exp_size, 2 * slot_cap
    )
    first_weights, second_weights = gate_tables(
        first_slot, local_of, gate_vals, first_ids, second_slot, second_ids, direct_index,
        row_count, direct, exp_local,
    )
    def weighted(weights, table, spec):
        high = weights.astype(jnp.bfloat16)
        low = (weights - high.astype(jnp.float32)).astype(jnp.bfloat16)
        return jnp.einsum(spec, high, table, preferred_element_type=jnp.float32) + jnp.einsum(
            spec, low, table, preferred_element_type=jnp.float32
        )

    first = weighted(first_weights, home_first, "pags,agsd->pd").reshape(
        seq_size, row_count, model_width
    )
    second = weighted(second_weights, home_second, "pgs,gsd->pd")
    expert_sum = first[0] + second[:row_count]
    for shift in range(1, seq_size):
        piece = first[shift]
        if shift == far:
            piece = piece + second[row_count:]
        expert_sum = expert_sum + seq_shift(
            piece.astype(jnp.bfloat16), -shift, seq_size
        ).astype(jnp.float32)
    return (mixed + expert_sum).astype(jnp.bfloat16).reshape(1, row_count, model_width)


def solution(mesh):
    in_specs = (
        P("exp", "seq", None),
        P("exp", "seq", None),
        P("seq", None),
        P(),
        P(),
        P("exp", None, None),
        P("exp", None, None, "seq"),
        P("exp", "seq", None),
    )
    out_specs = P("exp", "seq", None)

    return jax.shard_map(on_device, mesh=mesh, in_specs=in_specs, out_specs=out_specs, check_vma=False)
```

```python
import math

import jax
import jax.numpy as jnp
from jax import lax
from jax.sharding import PartitionSpec as P


H = 16
HD = 128
EXPERTS = 64


epsilon = 1e-05


def gate_weights(normed_rows, router_w, chosen):
    logits = jnp.dot(normed_rows, router_w, preferred_element_type=jnp.float32)
    match = chosen[:, :, None] == jnp.arange(logits.shape[1], dtype=jnp.int32)[None, None, :]
    picked = jnp.sum(jnp.where(match, logits[:, None, :], jnp.zeros((), logits.dtype)), axis=-1)
    squashed = jax.nn.sigmoid(picked)
    return squashed / jnp.sum(squashed, axis=-1, keepdims=True)


def slot_ranks(chosen, block_rows, experts):
    blocks = chosen.shape[0] // block_rows
    width = block_rows * chosen.shape[1]
    grouped = chosen.reshape(blocks, width)
    hits = (grouped[:, :, None] == jnp.arange(experts, dtype=jnp.int32)[None, None, :]).astype(
        jnp.bfloat16
    )
    lower = jnp.arange(width)[:, None] >= jnp.arange(width)[None, :]
    counts = jnp.einsum(
        "ij,bje->bie", lower.astype(jnp.bfloat16), hits, preferred_element_type=jnp.float32
    )
    ranks = jnp.sum(counts * hits.astype(jnp.float32), axis=-1) - 1
    return ranks.astype(jnp.int32).reshape(chosen.shape)


def expert_group(rows, gate_up, down):
    both = jnp.einsum("gsd,dxf->gsxf", rows, gate_up, preferred_element_type=jnp.float32)
    hidden = (jax.nn.silu(both[..., 0, :]) * both[..., 1, :]).astype(jnp.bfloat16)
    return jnp.einsum("gsf,fd->gsd", hidden, down, preferred_element_type=jnp.float32).astype(
        jnp.bfloat16
    )


def gate_tables(first_slot, local_of, gate_vals, first_ids, second_slot, second_ids, direct_index, row_count, direct, exp_local):
    first_weights = jnp.sum(
        jnp.where(
            (first_slot[:, :, None, None, None] == first_ids[None, None]) & (local_of == 0)[
                :, :, None, None, None
            ],
            gate_vals[:, :, None, None, None],
            0.0,
        ),
        axis=1,
    )
    second_gates = jnp.concatenate(
        [gate_vals[:row_count], gate_vals[direct : direct + row_count]], 0
    )
    second_weights = jnp.sum(
        jnp.where(
            (
                (jnp.concatenate([second_slot[:row_count], second_slot[direct : direct + row_count]], 0)[:, :, None, None] == second_ids[None, None])
                & (direct_index % exp_local == 1)[:, :, None, None]
            ),
            second_gates[:, :, None, None],
            0.0,
        ),
        axis=1,
    )

    return first_weights, second_weights


def seq_shift(x, shift, size):
    return lax.ppermute(x, "seq", [(i, (i + shift) % size) for i in range(size)])


def paired_shift(x, seq_size, exp_size, back):
    pairs = []
    for s in range(seq_size):
        for e in range(exp_size):
            step = 1 if e % 2 == 0 else -1
            if back:
                step = -step
            pairs.append((s * exp_size + e, ((s + step) % seq_size) * exp_size + e))
    return lax.ppermute(x, ("seq", "exp"), pairs)


def on_device(resid, qkv, w_out, norm_gain, router_w, expert_ids, w_gate_up, w_down):
    row_count = resid.shape[1]
    model_width = resid.shape[2]
    seq_size = lax.axis_size("seq")
    exp_size = lax.axis_size("exp")
    me = lax.axis_index("seq")
    seq_length = row_count * seq_size
    head_local = H // seq_size
    local_width = head_local * HD
    packed = qkv[0].reshape(row_count, 3, seq_size, local_width)
    pieces = []
    for shift in range(seq_size):
        target = (me + shift) % seq_size
        piece = lax.dynamic_index_in_dim(packed, target, axis=2, keepdims=False)
        pieces.append(piece if shift == 0 else seq_shift(piece, shift, seq_size))
    regrouped = jnp.stack(pieces, axis=0).reshape(seq_length, 3, local_width)
    queries = regrouped[:, 0].reshape(seq_length, head_local, HD)
    keys_all = regrouped[:, 1].reshape(seq_length, head_local, HD)
    values_all = regrouped[:, 2].reshape(seq_length, head_local, HD)
    scores = jnp.einsum(
        "qhd,khd->hqk", queries, keys_all, preferred_element_type=jnp.float32
    ) / math.sqrt(HD)
    weights = jax.nn.softmax(scores, axis=-1).astype(jnp.bfloat16)
    attended = jnp.einsum(
        "hqk,khd->qhd", weights, values_all, preferred_element_type=jnp.float32
    ).reshape(seq_length, local_width).astype(jnp.bfloat16)
    partial = jnp.dot(attended, w_out, preferred_element_type=jnp.float32).reshape(
        seq_size, row_count, model_width
    )
    projected = partial[0]
    for shift in range(1, seq_size):
        projected = projected + seq_shift(
            partial[shift].astype(jnp.bfloat16), -shift, seq_size
        ).astype(jnp.float32)
    mixed = resid[0].astype(jnp.float32) + projected
    meansq = jnp.mean(mixed * mixed, axis=-1, keepdims=True)
    normed = (mixed * lax.rsqrt(meansq + epsilon) * norm_gain).astype(jnp.bfloat16)
    exp_local = w_gate_up.shape[0]
    slot_cap = row_count // 8
    gathered = jnp.concatenate(
        [normed] + [seq_shift(normed, shift, seq_size) for shift in range(1, seq_size)], axis=0
    )
    far = seq_size // 2
    blocks_abs = (me - jnp.arange(seq_size, dtype=jnp.int32)) % seq_size
    chosen = jnp.take(expert_ids[0].reshape(seq_size, row_count, -1), blocks_abs, axis=0).reshape(
        seq_length, -1
    )
    gate_vals = gate_weights(gathered, router_w, chosen)
    ranks = slot_ranks(chosen, row_count, EXPERTS)
    owner = chosen // exp_local
    local_of = chosen % exp_local
    block_of = (jnp.arange(seq_length, dtype=jnp.int32) // row_count)[:, None]
    kind = block_of // far
    direct = row_count * far
    block_rows = gathered.reshape(seq_size, row_count, model_width)
    direct_rows = jnp.concatenate([block_rows[0], block_rows[far]], axis=0)
    direct_index = jnp.concatenate([chosen[:row_count], chosen[direct : direct + row_count]], 0)
    direct_ranks = jnp.concatenate([ranks[:row_count], ranks[direct : direct + row_count]], 0)
    direct_kind = (jnp.arange(2 * row_count, dtype=jnp.int32) // row_count)[:, None]
    direct_slot = (
        ((direct_index % exp_local) * exp_size + direct_index // exp_local) * 2 + direct_kind
    ) * slot_cap + direct_ranks
    grid = (exp_local, exp_size, 2 * slot_cap)
    slot_ids = jnp.arange(math.prod(grid), dtype=jnp.int32).reshape(grid)
    select = jnp.sum(
        (direct_slot[None, None, None, :, :] == slot_ids[..., None, None]).astype(jnp.bfloat16),
        axis=-1,
    )
    outgoing = jnp.einsum(
        "cgsp,pd->cgsd", select, direct_rows, preferred_element_type=jnp.float32
    ).astype(jnp.bfloat16)
    received = lax.all_to_all(outgoing[0], "exp", split_axis=0, concat_axis=0, tiled=True)
    forwarded = paired_shift(received, seq_size, exp_size, False)
    mine = expert_group(received, w_gate_up[0], w_down[0])
    theirs = expert_group(forwarded, w_gate_up[0], w_down[0])
    home_first = lax.all_to_all(
        jnp.stack([mine, theirs], axis=0), "exp", split_axis=1, concat_axis=1, tiled=True
    )
    received = lax.all_to_all(outgoing[1], "exp", split_axis=0, concat_axis=0, tiled=True)
    forwarded = paired_shift(received, seq_size, exp_size, False)
    mine = expert_group(received, w_gate_up[1], w_down[1])
    theirs = expert_group(forwarded, w_gate_up[1], w_down[1])
    returned = paired_shift(theirs, seq_size, exp_size, True)
    pair_sum = (mine.astype(jnp.float32) + returned.astype(jnp.float32)).astype(jnp.bfloat16)
    home_second = lax.all_to_all(pair_sum, "exp", split_axis=0, concat_axis=0, tiled=True)
    step = jnp.where(owner % 2 == 0, 1, seq_size - 1)
    neighbour_kind = jnp.where(block_of == step, 0, 1)
    is_direct = block_of % far == 0
    first_slot = (
        (jnp.where(is_direct, 0, 1) * exp_size + owner) * 2
        + jnp.where(is_direct, kind, neighbour_kind)
    ) * slot_cap + ranks
    first_ids = jnp.arange(2 * exp_size * 2 * slot_cap, dtype=jnp.int32).reshape(
        2, exp_size, 2 * slot_cap
    )
    second_slot = (owner * 2 + kind) * slot_cap + ranks
    second_ids = jnp.arange(exp_size * 2 * slot_cap, dtype=jnp.int32).reshape(
        exp_size, 2 * slot_cap
    )
    first_weights, second_weights = gate_tables(
        first_slot, local_of, gate_vals, first_ids, second_slot, second_ids, direct_index,
        row_count, direct, exp_local,
    )
    def weighted(weights, table, spec):
        high = weights.astype(jnp.bfloat16)
        low = (weights - high.astype(jnp.float32)).astype(jnp.bfloat16)
        return jnp.einsum(spec, high, table, preferred_element_type=jnp.float32) + jnp.einsum(
            spec, low, table, preferred_element_type=jnp.float32
        )

    first = weighted(first_weights, home_first, "pags,agsd->pd").reshape(
        seq_size, row_count, model_width
    )
    second_far = weighted(second_weights[row_count:], home_second, "pgs,gsd->pd")
    second_own = weighted(second_weights[:row_count], home_second, "pgs,gsd->pd")
    expert_sum = first[0] + second_own
    for shift in range(1, seq_size):
        piece = first[shift]
        if shift == far:
            piece = piece + second_far
        expert_sum = expert_sum + seq_shift(
            piece.astype(jnp.bfloat16), -shift, seq_size
        ).astype(jnp.float32)
    return (mixed + expert_sum).astype(jnp.bfloat16).reshape(1, row_count, model_width)


def solution(mesh):
    in_specs = (
        P("exp", "seq", None),
        P("exp", "seq", None),
        P("seq", None),
        P(),
        P(),
        P("exp", None, None),
        P("exp", None, None, "seq"),
        P("exp", "seq", None),
    )
    out_specs = P("exp", "seq", None)

    return jax.shard_map(on_device, mesh=mesh, in_specs=in_specs, out_specs=out_specs, check_vma=False)
```

```python
import math

import jax
import jax.numpy as jnp
from jax import lax
from jax.sharding import PartitionSpec as P


H = 16
HD = 128
EXPERTS = 64


epsilon = 1e-05


def gate_weights(normed_rows, router_w, chosen):
    logits = jnp.dot(normed_rows, router_w, preferred_element_type=jnp.float32)
    match = chosen[:, :, None] == jnp.arange(logits.shape[1], dtype=jnp.int32)[None, None, :]
    picked = jnp.sum(jnp.where(match, logits[:, None, :], jnp.zeros((), logits.dtype)), axis=-1)
    squashed = jax.nn.sigmoid(picked)
    return squashed / jnp.sum(squashed, axis=-1, keepdims=True)


def slot_ranks(chosen, block_rows, experts):
    blocks = chosen.shape[0] // block_rows
    width = block_rows * chosen.shape[1]
    grouped = chosen.reshape(blocks, width)
    hits = (grouped[:, :, None] == jnp.arange(experts, dtype=jnp.int32)[None, None, :]).astype(
        jnp.bfloat16
    )
    lower = jnp.arange(width)[:, None] >= jnp.arange(width)[None, :]
    counts = jnp.einsum(
        "ij,bje->bie", lower.astype(jnp.bfloat16), hits, preferred_element_type=jnp.float32
    )
    ranks = jnp.sum(counts * hits.astype(jnp.float32), axis=-1) - 1
    return ranks.astype(jnp.int32).reshape(chosen.shape)


def expert_group(rows, gate_up, down):
    both = jnp.einsum("gsd,dxf->gsxf", rows, gate_up, preferred_element_type=jnp.float32)
    hidden = (jax.nn.silu(both[..., 0, :]) * both[..., 1, :]).astype(jnp.bfloat16)
    return jnp.einsum("gsf,fd->gsd", hidden, down, preferred_element_type=jnp.float32).astype(
        jnp.bfloat16
    )


def gate_tables(first_slot, local_of, gate_vals, first_ids, second_slot, second_ids, direct_index, row_count, direct, exp_local):
    first_weights = jnp.sum(
        jnp.where(
            (first_slot[:, :, None, None, None] == first_ids[None, None]) & (local_of == 0)[
                :, :, None, None, None
            ],
            gate_vals[:, :, None, None, None],
            0.0,
        ),
        axis=1,
    )
    second_gates = jnp.concatenate(
        [gate_vals[:row_count], gate_vals[direct : direct + row_count]], 0
    )
    second_weights = jnp.sum(
        jnp.where(
            (
                (jnp.concatenate([second_slot[:row_count], second_slot[direct : direct + row_count]], 0)[:, :, None, None] == second_ids[None, None])
                & (direct_index % exp_local == 1)[:, :, None, None]
            ),
            second_gates[:, :, None, None],
            0.0,
        ),
        axis=1,
    )

    return first_weights, second_weights


def seq_shift(x, shift, size):
    return lax.ppermute(x, "seq", [(i, (i + shift) % size) for i in range(size)])


def paired_shift(x, seq_size, exp_size, back):
    pairs = []
    for s in range(seq_size):
        for e in range(exp_size):
            step = 1 if e % 2 == 0 else -1
            if back:
                step = -step
            pairs.append((s * exp_size + e, ((s + step) % seq_size) * exp_size + e))
    return lax.ppermute(x, ("seq", "exp"), pairs)


def on_device(resid, qkv, w_out, norm_gain, router_w, expert_ids, w_gate_up, w_down):
    row_count = resid.shape[1]
    model_width = resid.shape[2]
    seq_size = lax.axis_size("seq")
    exp_size = lax.axis_size("exp")
    me = lax.axis_index("seq")
    seq_length = row_count * seq_size
    head_local = H // seq_size
    local_width = head_local * HD
    packed = qkv[0].reshape(row_count, 3, seq_size, local_width)
    pieces = []
    for shift in range(seq_size):
        target = (me + shift) % seq_size
        piece = lax.dynamic_index_in_dim(packed, target, axis=2, keepdims=False)
        pieces.append(piece if shift == 0 else seq_shift(piece, shift, seq_size))
    regrouped = jnp.stack(pieces, axis=0).reshape(seq_length, 3, local_width)
    queries = regrouped[:, 0].reshape(seq_length, head_local, HD)
    keys_all = regrouped[:, 1].reshape(seq_length, head_local, HD)
    values_all = regrouped[:, 2].reshape(seq_length, head_local, HD)
    scores = jnp.einsum(
        "qhd,khd->hqk", queries, keys_all, preferred_element_type=jnp.float32
    ) / math.sqrt(HD)
    weights = jax.nn.softmax(scores, axis=-1).astype(jnp.bfloat16)
    attended = jnp.einsum(
        "hqk,khd->qhd", weights, values_all, preferred_element_type=jnp.float32
    ).reshape(seq_length, local_width).astype(jnp.bfloat16)
    partial = jnp.dot(attended, w_out, preferred_element_type=jnp.float32).reshape(
        seq_size, row_count, model_width
    )
    projected = partial[0]
    for shift in range(1, seq_size):
        projected = projected + seq_shift(
            partial[shift].astype(jnp.bfloat16), -shift, seq_size
        ).astype(jnp.float32)
    mixed = resid[0].astype(jnp.float32) + projected
    meansq = jnp.mean(mixed * mixed, axis=-1, keepdims=True)
    normed = (mixed * lax.rsqrt(meansq + epsilon) * norm_gain).astype(jnp.bfloat16)
    exp_local = w_gate_up.shape[0]
    slot_cap = row_count // 8
    gathered = jnp.concatenate(
        [normed] + [seq_shift(normed, shift, seq_size) for shift in range(1, seq_size)], axis=0
    )
    far = seq_size // 2
    blocks_abs = (me - jnp.arange(seq_size, dtype=jnp.int32)) % seq_size
    chosen = jnp.take(expert_ids[0].reshape(seq_size, row_count, -1), blocks_abs, axis=0).reshape(
        seq_length, -1
    )
    gate_vals = gate_weights(gathered, router_w, chosen)
    ranks = slot_ranks(chosen, row_count, EXPERTS)
    owner = chosen // exp_local
    local_of = chosen % exp_local
    block_of = (jnp.arange(seq_length, dtype=jnp.int32) // row_count)[:, None]
    kind = block_of // far
    direct = row_count * far
    block_rows = gathered.reshape(seq_size, row_count, model_width)
    direct_rows = jnp.concatenate([block_rows[0], block_rows[far]], axis=0)
    direct_index = jnp.concatenate([chosen[:row_count], chosen[direct : direct + row_count]], 0)
    direct_ranks = jnp.concatenate([ranks[:row_count], ranks[direct : direct + row_count]], 0)
    direct_kind = (jnp.arange(2 * row_count, dtype=jnp.int32) // row_count)[:, None]
    direct_slot = (
        ((direct_index % exp_local) * exp_size + direct_index // exp_local) * 2 + direct_kind
    ) * slot_cap + direct_ranks
    grid = (exp_local, exp_size, 2 * slot_cap)
    slot_ids = jnp.arange(math.prod(grid), dtype=jnp.int32).reshape(grid)
    select = jnp.sum(
        (direct_slot[None, None, None, :, :] == slot_ids[..., None, None]).astype(jnp.bfloat16),
        axis=-1,
    )
    outgoing = [
        jnp.einsum(
            "gsp,pd->gsd", select[local], direct_rows, preferred_element_type=jnp.float32
        ).astype(jnp.bfloat16)
        for local in range(exp_local)
    ]
    received = lax.all_to_all(outgoing[0], "exp", split_axis=0, concat_axis=0, tiled=True)
    forwarded = paired_shift(received, seq_size, exp_size, False)
    mine = expert_group(received, w_gate_up[0], w_down[0])
    theirs = expert_group(forwarded, w_gate_up[0], w_down[0])
    home_first = lax.all_to_all(
        jnp.stack([mine, theirs], axis=0), "exp", split_axis=1, concat_axis=1, tiled=True
    )
    received = lax.all_to_all(outgoing[1], "exp", split_axis=0, concat_axis=0, tiled=True)
    forwarded = paired_shift(received, seq_size, exp_size, False)
    mine = expert_group(received, w_gate_up[1], w_down[1])
    theirs = expert_group(forwarded, w_gate_up[1], w_down[1])
    returned = paired_shift(theirs, seq_size, exp_size, True)
    pair_sum = (mine.astype(jnp.float32) + returned.astype(jnp.float32)).astype(jnp.bfloat16)
    home_second = lax.all_to_all(pair_sum, "exp", split_axis=0, concat_axis=0, tiled=True)
    step = jnp.where(owner % 2 == 0, 1, seq_size - 1)
    neighbour_kind = jnp.where(block_of == step, 0, 1)
    is_direct = block_of % far == 0
    first_slot = (
        (jnp.where(is_direct, 0, 1) * exp_size + owner) * 2
        + jnp.where(is_direct, kind, neighbour_kind)
    ) * slot_cap + ranks
    first_ids = jnp.arange(2 * exp_size * 2 * slot_cap, dtype=jnp.int32).reshape(
        2, exp_size, 2 * slot_cap
    )
    second_slot = (owner * 2 + kind) * slot_cap + ranks
    second_ids = jnp.arange(exp_size * 2 * slot_cap, dtype=jnp.int32).reshape(
        exp_size, 2 * slot_cap
    )
    first_weights, second_weights = gate_tables(
        first_slot, local_of, gate_vals, first_ids, second_slot, second_ids, direct_index,
        row_count, direct, exp_local,
    )
    def weighted(weights, table, spec):
        high = weights.astype(jnp.bfloat16)
        low = (weights - high.astype(jnp.float32)).astype(jnp.bfloat16)
        return jnp.einsum(spec, high, table, preferred_element_type=jnp.float32) + jnp.einsum(
            spec, low, table, preferred_element_type=jnp.float32
        )

    first = weighted(first_weights, home_first, "pags,agsd->pd").reshape(
        seq_size, row_count, model_width
    )
    second = weighted(second_weights, home_second, "pgs,gsd->pd")
    expert_sum = first[0] + second[:row_count]
    for shift in range(1, seq_size):
        piece = first[shift]
        if shift == far:
            piece = piece + second[row_count:]
        expert_sum = expert_sum + seq_shift(
            piece.astype(jnp.bfloat16), -shift, seq_size
        ).astype(jnp.float32)
    return (mixed + expert_sum).astype(jnp.bfloat16).reshape(1, row_count, model_width)


def solution(mesh):
    in_specs = (
        P("exp", "seq", None),
        P("exp", "seq", None),
        P("seq", None),
        P(),
        P(),
        P("exp", None, None),
        P("exp", None, None, "seq"),
        P("exp", "seq", None),
    )
    out_specs = P("exp", "seq", None)

    return jax.shard_map(on_device, mesh=mesh, in_specs=in_specs, out_specs=out_specs, check_vma=False)
```

```python
import math

import jax
import jax.numpy as jnp
from jax import lax
from jax.sharding import PartitionSpec as P


H = 16
HD = 128
EXPERTS = 64


epsilon = 1e-05


def gate_weights(normed_rows, router_w, chosen):
    logits = jnp.dot(normed_rows, router_w, preferred_element_type=jnp.float32)
    match = chosen[:, :, None] == jnp.arange(logits.shape[1], dtype=jnp.int32)[None, None, :]
    picked = jnp.sum(jnp.where(match, logits[:, None, :], jnp.zeros((), logits.dtype)), axis=-1)
    squashed = jax.nn.sigmoid(picked)
    return squashed / jnp.sum(squashed, axis=-1, keepdims=True)


def slot_ranks(chosen, block_rows, experts):
    blocks = chosen.shape[0] // block_rows
    width = block_rows * chosen.shape[1]
    grouped = chosen.reshape(blocks, width)
    hits = (grouped[:, :, None] == jnp.arange(experts, dtype=jnp.int32)[None, None, :]).astype(
        jnp.bfloat16
    )
    lower = jnp.arange(width)[:, None] >= jnp.arange(width)[None, :]
    counts = jnp.einsum(
        "ij,bje->bie", lower.astype(jnp.bfloat16), hits, preferred_element_type=jnp.float32
    )
    ranks = jnp.sum(counts * hits.astype(jnp.float32), axis=-1) - 1
    return ranks.astype(jnp.int32).reshape(chosen.shape)


def hidden_of(rows, gate_up):
    both = jnp.einsum("gsd,dxf->gsxf", rows, gate_up, preferred_element_type=jnp.float32)
    return (jax.nn.silu(both[..., 0, :]) * both[..., 1, :]).astype(jnp.bfloat16)


def expert_group(rows, gate_up, down):
    both = jnp.einsum("gsd,dxf->gsxf", rows, gate_up, preferred_element_type=jnp.float32)
    hidden = (jax.nn.silu(both[..., 0, :]) * both[..., 1, :]).astype(jnp.bfloat16)
    return jnp.einsum("gsf,fd->gsd", hidden, down, preferred_element_type=jnp.float32).astype(
        jnp.bfloat16
    )


def gate_tables(first_slot, local_of, gate_vals, first_ids, second_slot, second_ids, direct_index, row_count, direct, exp_local):
    first_weights = jnp.sum(
        jnp.where(
            (first_slot[:, :, None, None, None] == first_ids[None, None]) & (local_of == 0)[
                :, :, None, None, None
            ],
            gate_vals[:, :, None, None, None],
            0.0,
        ),
        axis=1,
    )
    second_gates = jnp.concatenate(
        [gate_vals[:row_count], gate_vals[direct : direct + row_count]], 0
    )
    second_weights = jnp.sum(
        jnp.where(
            (
                (jnp.concatenate([second_slot[:row_count], second_slot[direct : direct + row_count]], 0)[:, :, None, None] == second_ids[None, None])
                & (direct_index % exp_local == 1)[:, :, None, None]
            ),
            second_gates[:, :, None, None],
            0.0,
        ),
        axis=1,
    )

    return first_weights, second_weights


def seq_shift(x, shift, size):
    return lax.ppermute(x, "seq", [(i, (i + shift) % size) for i in range(size)])


def paired_shift(x, seq_size, exp_size, back):
    pairs = []
    for s in range(seq_size):
        for e in range(exp_size):
            step = 1 if e % 2 == 0 else -1
            if back:
                step = -step
            pairs.append((s * exp_size + e, ((s + step) % seq_size) * exp_size + e))
    return lax.ppermute(x, ("seq", "exp"), pairs)


def on_device(resid, qkv, w_out, norm_gain, router_w, expert_ids, w_gate_up, w_down):
    row_count = resid.shape[1]
    model_width = resid.shape[2]
    seq_size = lax.axis_size("seq")
    exp_size = lax.axis_size("exp")
    me = lax.axis_index("seq")
    seq_length = row_count * seq_size
    head_local = H // seq_size
    local_width = head_local * HD
    packed = qkv[0].reshape(row_count, 3, seq_size, local_width)
    pieces = []
    for shift in range(seq_size):
        target = (me + shift) % seq_size
        piece = lax.dynamic_index_in_dim(packed, target, axis=2, keepdims=False)
        pieces.append(piece if shift == 0 else seq_shift(piece, shift, seq_size))
    regrouped = jnp.stack(pieces, axis=0).reshape(seq_length, 3, local_width)
    queries = regrouped[:, 0].reshape(seq_length, head_local, HD)
    keys_all = regrouped[:, 1].reshape(seq_length, head_local, HD)
    values_all = regrouped[:, 2].reshape(seq_length, head_local, HD)
    scores = jnp.einsum(
        "qhd,khd->hqk", queries, keys_all, preferred_element_type=jnp.float32
    ) / math.sqrt(HD)
    weights = jax.nn.softmax(scores, axis=-1).astype(jnp.bfloat16)
    attended = jnp.einsum(
        "hqk,khd->qhd", weights, values_all, preferred_element_type=jnp.float32
    ).reshape(seq_length, local_width).astype(jnp.bfloat16)
    partial = jnp.dot(attended, w_out, preferred_element_type=jnp.float32).reshape(
        seq_size, row_count, model_width
    )
    projected = partial[0]
    for shift in range(1, seq_size):
        projected = projected + seq_shift(
            partial[shift].astype(jnp.bfloat16), -shift, seq_size
        ).astype(jnp.float32)
    mixed = resid[0].astype(jnp.float32) + projected
    meansq = jnp.mean(mixed * mixed, axis=-1, keepdims=True)
    normed = (mixed * lax.rsqrt(meansq + epsilon) * norm_gain).astype(jnp.bfloat16)
    exp_local = w_gate_up.shape[0]
    slot_cap = row_count // 8
    gathered = jnp.concatenate(
        [normed] + [seq_shift(normed, shift, seq_size) for shift in range(1, seq_size)], axis=0
    )
    far = seq_size // 2
    blocks_abs = (me - jnp.arange(seq_size, dtype=jnp.int32)) % seq_size
    chosen = jnp.take(expert_ids[0].reshape(seq_size, row_count, -1), blocks_abs, axis=0).reshape(
        seq_length, -1
    )
    gate_vals = gate_weights(gathered, router_w, chosen)
    ranks = slot_ranks(chosen, row_count, EXPERTS)
    owner = chosen // exp_local
    local_of = chosen % exp_local
    block_of = (jnp.arange(seq_length, dtype=jnp.int32) // row_count)[:, None]
    kind = block_of // far
    direct = row_count * far
    block_rows = gathered.reshape(seq_size, row_count, model_width)
    direct_rows = jnp.concatenate([block_rows[0], block_rows[far]], axis=0)
    direct_index = jnp.concatenate([chosen[:row_count], chosen[direct : direct + row_count]], 0)
    direct_ranks = jnp.concatenate([ranks[:row_count], ranks[direct : direct + row_count]], 0)
    direct_kind = (jnp.arange(2 * row_count, dtype=jnp.int32) // row_count)[:, None]
    direct_slot = (
        ((direct_index % exp_local) * exp_size + direct_index // exp_local) * 2 + direct_kind
    ) * slot_cap + direct_ranks
    grid = (exp_local, exp_size, 2 * slot_cap)
    slot_ids = jnp.arange(math.prod(grid), dtype=jnp.int32).reshape(grid)
    select = jnp.sum(
        (direct_slot[None, None, None, :, :] == slot_ids[..., None, None]).astype(jnp.bfloat16),
        axis=-1,
    )
    outgoing = [
        jnp.einsum(
            "gsp,pd->gsd", select[local], direct_rows, preferred_element_type=jnp.float32
        ).astype(jnp.bfloat16)
        for local in range(exp_local)
    ]
    received = lax.all_to_all(outgoing[0], "exp", split_axis=0, concat_axis=0, tiled=True)
    forwarded = paired_shift(received, seq_size, exp_size, False)
    hidden_mine = hidden_of(received, w_gate_up[0])
    hidden_theirs = hidden_of(forwarded, w_gate_up[0])
    both_parts = jnp.einsum(
        "agsf,fd->agsd",
        jnp.stack([hidden_mine, hidden_theirs], axis=0),
        w_down[0],
        preferred_element_type=jnp.float32,
    ).astype(jnp.bfloat16)
    home_first = lax.all_to_all(both_parts, "exp", split_axis=1, concat_axis=1, tiled=True)
    received = lax.all_to_all(outgoing[1], "exp", split_axis=0, concat_axis=0, tiled=True)
    forwarded = paired_shift(received, seq_size, exp_size, False)
    mine = expert_group(received, w_gate_up[1], w_down[1])
    theirs = expert_group(forwarded, w_gate_up[1], w_down[1])
    returned = paired_shift(theirs, seq_size, exp_size, True)
    pair_sum = (mine.astype(jnp.float32) + returned.astype(jnp.float32)).astype(jnp.bfloat16)
    home_second = lax.all_to_all(pair_sum, "exp", split_axis=0, concat_axis=0, tiled=True)
    step = jnp.where(owner % 2 == 0, 1, seq_size - 1)
    neighbour_kind = jnp.where(block_of == step, 0, 1)
    is_direct = block_of % far == 0
    first_slot = (
        (jnp.where(is_direct, 0, 1) * exp_size + owner) * 2
        + jnp.where(is_direct, kind, neighbour_kind)
    ) * slot_cap + ranks
    first_ids = jnp.arange(2 * exp_size * 2 * slot_cap, dtype=jnp.int32).reshape(
        2, exp_size, 2 * slot_cap
    )
    second_slot = (owner * 2 + kind) * slot_cap + ranks
    second_ids = jnp.arange(exp_size * 2 * slot_cap, dtype=jnp.int32).reshape(
        exp_size, 2 * slot_cap
    )
    first_weights, second_weights = gate_tables(
        first_slot, local_of, gate_vals, first_ids, second_slot, second_ids, direct_index,
        row_count, direct, exp_local,
    )
    def weighted(weights, table, spec):
        high = weights.astype(jnp.bfloat16)
        low = (weights - high.astype(jnp.float32)).astype(jnp.bfloat16)
        return jnp.einsum(spec, high, table, preferred_element_type=jnp.float32) + jnp.einsum(
            spec, low, table, preferred_element_type=jnp.float32
        )

    first = weighted(first_weights, home_first, "pags,agsd->pd").reshape(
        seq_size, row_count, model_width
    )
    second = weighted(second_weights, home_second, "pgs,gsd->pd")
    expert_sum = first[0] + second[:row_count]
    for shift in range(1, seq_size):
        piece = first[shift]
        if shift == far:
            piece = piece + second[row_count:]
        expert_sum = expert_sum + seq_shift(
            piece.astype(jnp.bfloat16), -shift, seq_size
        ).astype(jnp.float32)
    return (mixed + expert_sum).astype(jnp.bfloat16).reshape(1, row_count, model_width)


def solution(mesh):
    in_specs = (
        P("exp", "seq", None),
        P("exp", "seq", None),
        P("seq", None),
        P(),
        P(),
        P("exp", None, None),
        P("exp", None, None, "seq"),
        P("exp", "seq", None),
    )
    out_specs = P("exp", "seq", None)

    return jax.shard_map(on_device, mesh=mesh, in_specs=in_specs, out_specs=out_specs, check_vma=False)
```
